512 devices in a mesh: dp: 32 (over y, x), section: 4 (over z_hi), space: 4 (over z_lo, core).
Axes of the slice: x: 4, y: 8, z: 8 (z_hi: 4, z_lo: 2; z = z_hi * 2 + z_lo), core: 2. Of those that a mesh axis runs over, the one named last changes fastest.
Arguments:
- images: bfloat16 [64, 4, 64, 256], P('dp', 'space'), may hold values from -6 to 6
- steps: int32 [64], P('dp'), may hold values from 0 to 999
- out_grad: bfloat16 [64, 4, 64, 256], P('dp', 'space'), may hold values from -0.125 to 0.125
- conv_weight: bfloat16 [4, 3, 3, 256, 256], P('section'), may hold values from -0.125 to 0.125
- gn_gain: float32 [4, 256], P('section'), may hold values from 0.5 to 2
- emb_weight: bfloat16 [4, 256, 512], P('section'), may hold values from -0.375 to 0.375
Outputs:
- grad_conv: float32 [4, 3, 3, 256, 256], P('section')
- grad_gain: float32 [4, 256], P('section')
- grad_emb: float32 [4, 256, 512], P('section')
The draws below stay inside these ranges and needn't reach their ends.
All inputs are finite; a program needn't handle non-finite values.
Results may differ from the reference program's by a relative error of at most 0.0064.
Values may be sent and summed in bfloat16 or wider, within the bound.
No kernel may reach another device: no remote copies, remote signals or barrier semaphores. Data moves between devices by JAX's collectives and lax.ppermute only.
A program may use at most 64 MiB of HBM per device.

```python
import math
import jax
import jax.numpy as jnp
from jax import lax

C = 256
G = 32
FREQ = 256
MICRO = 2
IMGS = 1
COLS = 64
SECTIONS = 4
BATCH = 64
H = 4
N_DP = 32


def touch_ends(values, rng, smallest, largest):
    place = [jax.random.randint(jax.random.fold_in(rng, axis), (), 0, length) for axis, length in enumerate(values.shape)]
    longest = values.shape.index(max(values.shape))
    next_to = place[:longest] + [(place[longest] + 1) % values.shape[longest]] + place[longest + 1:]
    return values.at[tuple(place)].set(smallest).at[tuple(next_to)].set(largest)


def shard_levels(key, dims, shards, smallest, top_value):
    def one(position, parts):
        draws = jax.random.uniform(jax.random.fold_in(jax.random.fold_in(key, 6), position), (parts,), jnp.float32, smallest / len(shards), top_value / len(shards))
        return jnp.repeat(jnp.exp(draws), dims[position] // parts).reshape((-1,) + (1,) * (len(dims) - position - 1))

    loudness = one(*shards[0])
    for cut in shards[1:]:
        loudness = loudness * one(*cut)
    return loudness


def scatter_about(key, dims, scale, limit, shards=(), held_as=jnp.bfloat16):
    entries = scale * jax.random.normal(key, dims, jnp.float32)
    if shards:
        entries = entries * shard_levels(key, dims, shards, -0.22, 0.18)
    return jnp.clip(entries, -limit, limit).astype(held_as)


def setup_inputs(seed: int = 0) -> dict:
    splits = jax.random.split(jax.random.key(seed), 7)
    return {
        "images": scatter_about(splits[0], (BATCH, H, COLS, C), 1.0, 6.0, ((0, 32), (1, 4))),
        "steps": touch_ends(jax.random.randint(splits[1], (BATCH,), 0, 1000), jax.random.fold_in(splits[1], 1), 0, 999).astype(jnp.int32),
        "out_grad": scatter_about(splits[2], (BATCH, H, COLS, C), ((BATCH * H * COLS) ** -0.5), 0.125, ((0, 32), (1, 4))),
        "conv_weight": scatter_about(splits[3], (SECTIONS, 3, 3, C, C), (9 * C) ** -0.5, 0.125, ((0, 4),)),
        "gn_gain": jnp.clip(jnp.exp(math.log(2.0) - 1.3862944 * jax.random.uniform(splits[4], (SECTIONS, C), jnp.float32) ** shard_levels(splits[4], (SECTIONS, C), ((0, 4),), -0.2, 0.2)), 0.5, 2.0),
        "emb_weight": scatter_about(splits[5], (SECTIONS, FREQ, 2 * C), FREQ ** -0.5, 0.375, ((0, 4),)),
    }


EPS = 1e-05

def sinusoid(timesteps, feature_n):
    half_n = feature_n // 2
    freqs = jnp.exp(-math.log(10000.0) * jnp.arange(half_n, dtype=jnp.float32) / half_n)
    angles = timesteps.astype(jnp.float32)[:, None] * freqs[None, :]
    return jnp.concatenate([jnp.cos(angles), jnp.sin(angles)], axis=1)

def group_sums(tensor, groups):
    batch_n, height_n, width_n, channels = tensor.shape
    split = tensor.reshape(batch_n, height_n, width_n, groups, channels // groups)
    return (lax.optimization_barrier(jnp.sum(split, axis=(1, 2, 4))), lax.optimization_barrier(jnp.sum(split * split, axis=(1, 2, 4))))

def spread(values, channels):
    return jnp.repeat(values, channels // values.shape[1], axis=1)[:, None, None, :]

def normalize(tensor, first_sum, square_sum, gains, scales, shifts, cell_count):
    channels = tensor.shape[3]
    average = first_sum / cell_count
    inverse = lax.rsqrt(square_sum / cell_count - average * average + EPS)
    normed = (tensor - spread(average, channels)) * spread(inverse, channels) * gains
    return normed * (1.0 + scales[:, None, None, :]) + shifts[:, None, None, :]

def patches(padded, height_n, width_n):
    return jnp.concatenate([padded[:, vertical:vertical + height_n, lateral:lateral + width_n, :] for vertical in range(3) for lateral in range(3)], axis=3)

def convolve(padded, matrix):
    batch_n, height_p, width_p, channels = padded.shape
    flat = patches(padded, height_p - 2, width_p - 2).reshape(-1, 9 * channels)
    return jnp.dot(flat, matrix, preferred_element_type=jnp.float32).reshape(batch_n, height_p - 2, width_p - 2, matrix.shape[1])

def flip_weight(weight):
    channels = weight.shape[2]
    return jnp.transpose(weight[::-1, ::-1], (0, 1, 3, 2)).reshape(9 * channels, channels)

def silu_slope(pre_act):
    sigmoid_v = jax.nn.sigmoid(pre_act)
    return sigmoid_v * (1.0 + pre_act * (1.0 - sigmoid_v))

def pad_both(tensor):
    return jnp.pad(tensor, ((0, 0), (1, 1), (1, 1), (0, 0)))

def norm_backward(tensor, first_sum, square_sum, gains, scales, shifts, cell_count, d_pre):

    def mapping(tensor_v, first_v, square_v, gains_v, scales_v, shifts_v):
        return normalize(tensor_v, first_v, square_v, gains_v, scales_v, shifts_v, cell_count)
    _, pull_back = jax.vjp(mapping, tensor, first_sum, square_sum, gains, scales, shifts)
    return pull_back(d_pre)

def block_forward(inputs, weight, gains, emb_matrix, features, cell_count):
    tensor = inputs.astype(jnp.float32)
    channels = tensor.shape[3]
    first_sum, square_sum = group_sums(tensor, G)
    embedded = jnp.dot(features, emb_matrix.astype(jnp.float32), precision=lax.Precision.HIGHEST)
    scales = embedded[:, :channels]
    shifts = embedded[:, channels:]
    pre_act = normalize(tensor, first_sum, square_sum, gains, scales, shifts, cell_count)
    activation = jax.nn.silu(pre_act).astype(jnp.bfloat16)
    padded = pad_both(activation)
    conv_out = convolve(padded, weight.reshape(9 * channels, channels))
    output = (tensor + conv_out).astype(jnp.bfloat16)
    return (output, (tensor, first_sum, square_sum, scales, shifts, pre_act, padded))

def block_backward(upstream, saved, weight, gains, cell_count):
    tensor, first_sum, square_sum, scales, shifts, pre_act, padded = saved
    batch_n, height_n, width_n, channels = tensor.shape
    flat_patch = patches(padded, height_n, width_n).reshape(-1, 9 * channels)
    d_weight = jnp.dot(flat_patch.T, upstream.reshape(-1, channels), preferred_element_type=jnp.float32)
    d_act = convolve(pad_both(upstream), flip_weight(weight))
    d_pre = d_act * silu_slope(pre_act)
    d_tensor, d_first, d_square, d_gains, d_scales, d_shifts = norm_backward(tensor, first_sum, square_sum, gains, scales, shifts, cell_count, d_pre)
    d_tensor = d_tensor + spread(d_first, channels) + 2.0 * tensor * spread(d_square, channels)
    d_input = (upstream.astype(jnp.float32) + d_tensor).astype(jnp.bfloat16)
    return (d_input, d_weight, d_gains, jnp.concatenate([d_scales, d_shifts], axis=1))

def reference(images, steps, out_grad, conv_weight, gn_gain, emb_weight):
    group_n = MICRO * IMGS
    shape = (N_DP, group_n, H, COLS, C)
    cell_count = H * COLS * (C // G)

    def one_group(totals, pieces):
        group_images, group_steps, group_grad = pieces
        features = sinusoid(group_steps, FREQ)
        stash = []
        current = group_images
        for section_no in range(SECTIONS - 1):
            current, saved = block_forward(current, conv_weight[section_no], gn_gain[section_no], emb_weight[section_no], features, cell_count)
            stash.append((current, saved))
        joined = (current.astype(jnp.float32) + stash[0][0].astype(jnp.float32)).astype(jnp.bfloat16)
        final_out, final_saved = block_forward(joined, conv_weight[3], gn_gain[3], emb_weight[3], features, cell_count)
        back_three = block_backward(group_grad, final_saved, conv_weight[3], gn_gain[3], cell_count)
        back_two = block_backward(back_three[0], stash[2][1], conv_weight[2], gn_gain[2], cell_count)
        back_one = block_backward(back_two[0], stash[1][1], conv_weight[1], gn_gain[1], cell_count)
        start_zero = (back_one[0].astype(jnp.float32) + back_three[0].astype(jnp.float32)).astype(jnp.bfloat16)
        back_zero = block_backward(start_zero, stash[0][1], conv_weight[0], gn_gain[0], cell_count)
        records = [back_zero, back_one, back_two, back_three]
        conv_sum = jnp.stack([record[1] for record in records]).reshape(SECTIONS, 3, 3, C, C)
        gain_sum = jnp.stack([record[2] for record in records])
        emb_sum = jnp.stack([jnp.dot(features.T, record[3], precision=lax.Precision.HIGHEST) for record in records])
        return ((totals[0] + conv_sum, totals[1] + gain_sum, totals[2] + emb_sum), None)
    start = (jnp.zeros((SECTIONS, 3, 3, C, C), jnp.float32), jnp.zeros((SECTIONS, C), jnp.float32), jnp.zeros((SECTIONS, FREQ, 2 * C), jnp.float32))
    totals, _ = lax.scan(one_group, start, (images.reshape(shape), steps.reshape(N_DP, group_n), out_grad.reshape(shape)))
    return (totals[0], totals[1], totals[2])
```

```python
import math

import jax
import jax.numpy as jnp
from jax import lax
from jax.sharding import Mesh, PartitionSpec as P

G = 32
FREQ = 256
MICRO = 2


EPS = 1e-05


def from_behind(value, axis, steps):
    count = lax.axis_size(axis)
    initial, last = (max(0, -steps), min(count, count - steps))
    return lax.ppermute(value, axis, [(source, source + steps) for source in range(initial, last)])


def extended(shard, sides, width):
    for axis, dim in sides:
        size, length = (lax.axis_size(axis), shard.shape[dim])
        up = [(i, (i + 1) % size) for i in range(size - 1)]
        down = [(j, i) for i, j in up]
        last = lax.slice_in_dim(shard, length - width, length, axis=dim)
        initial = lax.slice_in_dim(shard, 0, width, axis=dim)
        before = lax.ppermute(last, axis, up)
        after = lax.ppermute(initial, axis, down)
        shard = jnp.concatenate([before, shard, after], axis=dim)
    return shard


def sinusoid(timesteps, feature_n):
    half_n = feature_n // 2
    freqs = jnp.exp(-math.log(10000.0) * jnp.arange(half_n, dtype=jnp.float32) / half_n)
    angles = timesteps.astype(jnp.float32)[:, None] * freqs[None, :]
    return jnp.concatenate([jnp.cos(angles), jnp.sin(angles)], axis=1)


def group_sums(tensor, groups):
    batch_n, height_n, width_n, channels = tensor.shape
    split = tensor.reshape(batch_n, height_n, width_n, groups, channels // groups)
    return (jnp.sum(split, axis=(1, 2, 4)), jnp.sum(split * split, axis=(1, 2, 4)))


def spread(values, channels):
    return jnp.repeat(values, channels // values.shape[1], axis=1)[:, None, None, :]


def normalize(tensor, first_sum, square_sum, gains, scales, shifts, cell_count):
    channels = tensor.shape[3]
    average = first_sum / cell_count
    inverse = lax.rsqrt(square_sum / cell_count - average * average + EPS)
    normed = (tensor - spread(average, channels)) * spread(inverse, channels) * gains
    return normed * (1.0 + scales[:, None, None, :]) + shifts[:, None, None, :]


def patches(padded, height_n, width_n):
    return jnp.concatenate(
        [
            padded[:, vertical : vertical + height_n, lateral : lateral + width_n, :]
            for vertical in range(3)
            for lateral in range(3)
        ],
        axis=3,
    )


def convolve(padded, matrix):
    batch_n, height_p, width_p, channels = padded.shape
    flat = patches(padded, height_p - 2, width_p - 2).reshape(-1, 9 * channels)
    return jnp.dot(flat, matrix, preferred_element_type=jnp.float32).reshape(
        batch_n, height_p - 2, width_p - 2, matrix.shape[1]
    )


def flip_weight(weight):
    channels = weight.shape[2]
    return jnp.transpose(weight[::-1, ::-1], (0, 1, 3, 2)).reshape(9 * channels, channels)


def silu_slope(pre_act):
    sigmoid_v = jax.nn.sigmoid(pre_act)
    return sigmoid_v * (1.0 + pre_act * (1.0 - sigmoid_v))


def pad_columns(tensor):
    return jnp.pad(tensor, ((0, 0), (0, 0), (1, 1), (0, 0)))


def pick(stacked, index):
    return lax.dynamic_index_in_dim(stacked, index, 0, keepdims=False)


def norm_backward(tensor, first_sum, square_sum, gains, scales, shifts, cell_count, d_pre):

    def mapping(tensor_v, first_v, square_v, gains_v, scales_v, shifts_v):
        return normalize(tensor_v, first_v, square_v, gains_v, scales_v, shifts_v, cell_count)

    _, pull_back = jax.vjp(mapping, tensor, first_sum, square_sum, gains, scales, shifts)
    return pull_back(d_pre)


def pad_both(tensor):
    return jnp.pad(tensor, ((0, 0), (1, 1), (1, 1), (0, 0)))


def block_forward(inputs, flat_weight, gains, scales, shifts, cell_count):
    tensor = inputs.astype(jnp.float32)
    first_sum, square_sum = group_sums(tensor, G)
    pre_act = normalize(tensor, first_sum, square_sum, gains, scales, shifts, cell_count)
    activation = jax.nn.silu(pre_act).astype(jnp.bfloat16)
    padded = pad_both(activation)
    output = (tensor + convolve(padded, flat_weight)).astype(jnp.bfloat16)
    return output, (first_sum, square_sum, padded)


def block_backward(upstream, inputs, saved, flipped, gains, scales, shifts, cell_count):
    first_sum, square_sum, _ = saved
    channels = inputs.shape[3]
    tensor = inputs.astype(jnp.float32)
    pre_act = normalize(tensor, first_sum, square_sum, gains, scales, shifts, cell_count)
    d_act = convolve(pad_both(upstream), flipped)
    d_pre = d_act * silu_slope(pre_act)
    d_tensor, d_first, d_square, d_gains, d_scales, d_shifts = norm_backward(
        tensor, first_sum, square_sum, gains, scales, shifts, cell_count, d_pre
    )
    d_tensor = d_tensor + spread(d_first, channels) + 2.0 * tensor * spread(d_square, channels)
    d_input = (upstream.astype(jnp.float32) + d_tensor).astype(jnp.bfloat16)
    return d_input, (d_gains, d_scales, d_shifts)


def keep(flag, new, old):
    return jax.tree.map(lambda a, b: jnp.where(flag, a, b), new, old)


def per_device(images, steps, out_grad, conv_weight, gn_gain, emb_weight):
    section_count = lax.axis_size("section")
    section_no = lax.axis_index("section")
    images = lax.all_gather(images, "space", axis=1, tiled=True)
    out_grad = lax.all_gather(out_grad, "space", axis=1, tiled=True)
    row_count = images.shape[1]
    col_count = images.shape[2]
    channels = images.shape[3]
    cell_count = row_count * col_count * (channels // G)
    weight = conv_weight[0]
    flat_weight = weight.reshape(9 * channels, channels)
    flipped = flip_weight(weight)
    gains = gn_gain[0]
    features = sinusoid(steps, FREQ)
    embedded = jnp.dot(features, emb_weight[0].astype(jnp.float32), precision=lax.Precision.HIGHEST)
    scales = embedded[:, :channels]
    shifts = embedded[:, channels:]
    last = section_count - 1
    carried = images
    kept = None
    for moment in range(section_count):
        inputs = images
        if moment > 0:
            inputs = lax.ppermute(carried, "section", [(moment - 1, moment)])
        if moment == last:
            inputs = (inputs.astype(jnp.float32) + skip.astype(jnp.float32)).astype(jnp.bfloat16)
        output, saved = block_forward(inputs, flat_weight, gains, scales, shifts, cell_count)
        if moment == 0:
            skip = lax.ppermute(output, "section", [(0, last)])
        state = (inputs, saved)
        kept = state if kept is None else keep(section_no == moment, state, kept)
        carried = output
    kept_in, kept_saved = kept
    carried = out_grad
    kept = None
    for moment in range(section_count):
        active = last - moment
        upstream = out_grad
        if moment > 0:
            upstream = lax.ppermute(carried, "section", [(active + 1, active)])
        if active == 0:
            upstream = (upstream.astype(jnp.float32) + skip_grad.astype(jnp.float32)).astype(
                jnp.bfloat16
            )
        d_input, pieces = block_backward(
            upstream, kept_in, kept_saved, flipped, gains, scales, shifts, cell_count
        )
        if moment == 0:
            skip_grad = lax.ppermute(d_input, "section", [(last, 0)])
        state = (upstream, pieces)
        kept = state if kept is None else keep(section_no == active, state, kept)
        carried = d_input
    kept_up, (d_gains, d_scales, d_shifts) = kept
    space_count = lax.axis_size("space")
    space_no = lax.axis_index("space")
    patch_rows = 9 * channels // space_count
    flat_patch = patches(kept_saved[2], row_count, col_count).reshape(-1, 9 * channels)
    own_patch = lax.dynamic_slice_in_dim(flat_patch, space_no * patch_rows, patch_rows, axis=1)
    weight_grad = jnp.dot(
        own_patch.T, kept_up.reshape(-1, channels), preferred_element_type=jnp.float32
    )
    emb_rows = FREQ // space_count
    own_features = lax.dynamic_slice_in_dim(features, space_no * emb_rows, emb_rows, axis=1)
    emb_grad = jnp.dot(
        own_features.T,
        jnp.concatenate([d_scales, d_shifts], axis=1),
        precision=lax.Precision.HIGHEST,
    )
    return reduce_grads(weight_grad, d_gains, emb_grad)


def reduce_grads(weight_grad, gain_grad, emb_grad):
    channels = gain_grad.shape[0]
    parts = [weight_grad, emb_grad.reshape(-1, channels), gain_grad[None]]
    rows = sum(part.shape[0] for part in parts)
    devices = lax.axis_size("dx") * lax.axis_size("dy")
    padded_rows = -(-rows // (8 * devices)) * 8 * devices
    parts.append(jnp.zeros((padded_rows - rows, channels), jnp.float32))
    flat = jnp.concatenate(parts, axis=0)
    for axis in ("dx", "dy"):
        flat = lax.psum_scatter(flat, axis, scatter_dimension=0, tiled=True)
    for axis in ("dy", "dx"):
        flat = lax.all_gather(flat, axis, axis=0, tiled=True)
    flat = lax.all_gather(flat, "space", axis=0)
    space_count = flat.shape[0]
    weight_rows = weight_grad.shape[0]
    emb_rows = emb_grad.size // channels
    conv = flat[:, :weight_rows].reshape(1, 3, 3, channels, channels)
    emb = flat[:, weight_rows : weight_rows + emb_rows].reshape(1, emb_grad.shape[0] * space_count, -1)
    gain = flat[0, weight_rows + emb_rows][None]
    return (conv, gain, emb)


def solution(mesh):
    dp_n = mesh.shape["dp"]
    dx_n = 4 if dp_n % 4 == 0 else 1
    mesh = Mesh(
        mesh.devices.reshape(dp_n // dx_n, dx_n, *mesh.devices.shape[1:]),
        ("dy", "dx", "section", "space"),
    )
    data = ("dy", "dx")
    in_specs = (
        P(data, "space", None, None),
        P(data),
        P(data, "space", None, None),
        P("section", None, None, None, None),
        P("section", None),
        P("section", None, None),
    )
    out_specs = (P("section", None, None, None, None), P("section", None), P("section", None, None))
    return jax.shard_map(
        per_device, mesh=mesh, in_specs=in_specs, out_specs=out_specs, check_vma=False
    )
```

```python
import math

import jax
import jax.numpy as jnp
from jax import lax
from jax.sharding import Mesh, PartitionSpec as P

G = 32
FREQ = 256
MICRO = 2


EPS = 1e-05


def from_behind(value, axis, steps):
    count = lax.axis_size(axis)
    initial, last = (max(0, -steps), min(count, count - steps))
    return lax.ppermute(value, axis, [(source, source + steps) for source in range(initial, last)])


def extended(shard, sides, width):
    for axis, dim in sides:
        size, length = (lax.axis_size(axis), shard.shape[dim])
        up = [(i, (i + 1) % size) for i in range(size - 1)]
        down = [(j, i) for i, j in up]
        last = lax.slice_in_dim(shard, length - width, length, axis=dim)
        initial = lax.slice_in_dim(shard, 0, width, axis=dim)
        before = lax.ppermute(last, axis, up)
        after = lax.ppermute(initial, axis, down)
        shard = jnp.concatenate([before, shard, after], axis=dim)
    return shard


def sinusoid(timesteps, feature_n):
    half_n = feature_n // 2
    freqs = jnp.exp(-math.log(10000.0) * jnp.arange(half_n, dtype=jnp.float32) / half_n)
    angles = timesteps.astype(jnp.float32)[:, None] * freqs[None, :]
    return jnp.concatenate([jnp.cos(angles), jnp.sin(angles)], axis=1)


def group_sums(tensor, groups):
    batch_n, height_n, width_n, channels = tensor.shape
    split = tensor.reshape(batch_n, height_n, width_n, groups, channels // groups)
    return (jnp.sum(split, axis=(1, 2, 4)), jnp.sum(split * split, axis=(1, 2, 4)))


def spread(values, channels):
    return jnp.repeat(values, channels // values.shape[1], axis=1)[:, None, None, :]


def normalize(tensor, first_sum, square_sum, gains, scales, shifts, cell_count):
    channels = tensor.shape[3]
    average = first_sum / cell_count
    inverse = lax.rsqrt(square_sum / cell_count - average * average + EPS)
    normed = (tensor - spread(average, channels)) * spread(inverse, channels) * gains
    return normed * (1.0 + scales[:, None, None, :]) + shifts[:, None, None, :]


def patches(padded, height_n, width_n):
    return jnp.concatenate(
        [
            padded[:, vertical : vertical + height_n, lateral : lateral + width_n, :]
            for vertical in range(3)
            for lateral in range(3)
        ],
        axis=3,
    )


def convolve(padded, matrix):
    batch_n, height_p, width_p, channels = padded.shape
    flat = patches(padded, height_p - 2, width_p - 2).reshape(-1, 9 * channels)
    return jnp.dot(flat, matrix, preferred_element_type=jnp.float32).reshape(
        batch_n, height_p - 2, width_p - 2, matrix.shape[1]
    )


def flip_weight(weight):
    channels = weight.shape[2]
    return jnp.transpose(weight[::-1, ::-1], (0, 1, 3, 2)).reshape(9 * channels, channels)


def silu_slope(pre_act):
    sigmoid_v = jax.nn.sigmoid(pre_act)
    return sigmoid_v * (1.0 + pre_act * (1.0 - sigmoid_v))


def pad_columns(tensor):
    return jnp.pad(tensor, ((0, 0), (0, 0), (1, 1), (0, 0)))


def pick(stacked, index):
    return lax.dynamic_index_in_dim(stacked, index, 0, keepdims=False)


def norm_backward(tensor, first_sum, square_sum, gains, scales, shifts, cell_count, d_pre):

    def mapping(tensor_v, first_v, square_v, gains_v, scales_v, shifts_v):
        return normalize(tensor_v, first_v, square_v, gains_v, scales_v, shifts_v, cell_count)

    _, pull_back = jax.vjp(mapping, tensor, first_sum, square_sum, gains, scales, shifts)
    return pull_back(d_pre)


def pad_both(tensor):
    return jnp.pad(tensor, ((0, 0), (1, 1), (1, 1), (0, 0)))


def block_forward(inputs, flat_weight, gains, scales, shifts, cell_count):
    tensor = inputs.astype(jnp.float32)
    first_sum, square_sum = group_sums(tensor, G)
    pre_act = normalize(tensor, first_sum, square_sum, gains, scales, shifts, cell_count)
    activation = jax.nn.silu(pre_act).astype(jnp.bfloat16)
    padded = pad_both(activation)
    output = (tensor + convolve(padded, flat_weight)).astype(jnp.bfloat16)
    return output, (first_sum, square_sum, padded)


def block_backward(upstream, inputs, saved, flipped, gains, scales, shifts, cell_count):
    first_sum, square_sum, _ = saved
    channels = inputs.shape[3]
    tensor = inputs.astype(jnp.float32)
    pre_act = normalize(tensor, first_sum, square_sum, gains, scales, shifts, cell_count)
    d_act = convolve(pad_both(upstream), flipped)
    d_pre = d_act * silu_slope(pre_act)
    d_tensor, d_first, d_square, d_gains, d_scales, d_shifts = norm_backward(
        tensor, first_sum, square_sum, gains, scales, shifts, cell_count, d_pre
    )
    d_tensor = d_tensor + spread(d_first, channels) + 2.0 * tensor * spread(d_square, channels)
    d_input = (upstream.astype(jnp.float32) + d_tensor).astype(jnp.bfloat16)
    return d_input, (d_gains, d_scales, d_shifts)


def keep(flag, new, old):
    return jax.tree.map(lambda a, b: jnp.where(flag, a, b), new, old)


def per_device(images, steps, out_grad, conv_weight, gn_gain, emb_weight):
    section_count = lax.axis_size("section")
    section_no = lax.axis_index("section")
    images = lax.all_gather(images, "space", axis=1, tiled=True)
    out_grad = lax.all_gather(out_grad, "space", axis=1, tiled=True)
    row_count = images.shape[1]
    col_count = images.shape[2]
    channels = images.shape[3]
    cell_count = row_count * col_count * (channels // G)
    weight = conv_weight[0]
    flat_weight = weight.reshape(9 * channels, channels)
    flipped = flip_weight(weight)
    gains = gn_gain[0]
    features = sinusoid(steps, FREQ)
    embedded = jnp.dot(features, emb_weight[0].astype(jnp.float32), precision=lax.Precision.HIGHEST)
    scales = embedded[:, :channels]
    shifts = embedded[:, channels:]
    last = section_count - 1
    carried = images
    kept = None
    for moment in range(section_count):
        inputs = images
        if moment > 0:
            inputs = lax.ppermute(carried, "section", [(moment - 1, moment)])
        if moment == last:
            inputs = (inputs.astype(jnp.float32) + skip.astype(jnp.float32)).astype(jnp.bfloat16)
        output, saved = block_forward(inputs, flat_weight, gains, scales, shifts, cell_count)
        if moment == 0:
            skip = lax.ppermute(output, "section", [(0, last)])
        state = (inputs, saved)
        kept = state if kept is None else keep(section_no == moment, state, kept)
        carried = output
    kept_in, kept_saved = kept
    carried = out_grad
    kept = None
    for moment in range(section_count):
        active = last - moment
        upstream = out_grad
        if moment > 0:
            upstream = lax.ppermute(carried, "section", [(active + 1, active)])
        if active == 0:
            upstream = (upstream.astype(jnp.float32) + skip_grad.astype(jnp.float32)).astype(
                jnp.bfloat16
            )
        d_input, pieces = block_backward(
            upstream, kept_in, kept_saved, flipped, gains, scales, shifts, cell_count
        )
        if moment == 0:
            skip_grad = lax.ppermute(d_input, "section", [(last, 0)])
        state = (upstream, pieces)
        kept = state if kept is None else keep(section_no == active, state, kept)
        carried = d_input
    kept_up, (d_gains, d_scales, d_shifts) = kept
    space_count = lax.axis_size("space")
    space_no = quarter_of(lax.axis_index("space"), space_count)
    patch_rows = 9 * channels // space_count
    flat_patch = patches(kept_saved[2], row_count, col_count).reshape(-1, 9 * channels)
    own_patch = lax.dynamic_slice_in_dim(flat_patch, space_no * patch_rows, patch_rows, axis=1)
    weight_grad = jnp.dot(
        own_patch.T, kept_up.reshape(-1, channels), preferred_element_type=jnp.float32
    )
    emb_rows = FREQ // space_count
    own_features = lax.dynamic_slice_in_dim(features, space_no * emb_rows, emb_rows, axis=1)
    emb_grad = jnp.dot(
        own_features.T,
        jnp.concatenate([d_scales, d_shifts], axis=1),
        precision=lax.Precision.HIGHEST,
    )
    return reduce_grads(weight_grad, d_gains, emb_grad)


def butterfly_scatter(flat, axis):
    count = lax.axis_size(axis)
    index = lax.axis_index(axis)
    step = 1
    while step < count:
        bit = (index // step) % 2
        half = flat.shape[0] // 2
        kept = lax.dynamic_slice_in_dim(flat, bit * half, half, 0)
        sent = lax.dynamic_slice_in_dim(flat, (1 - bit) * half, half, 0)
        flat = kept + lax.ppermute(sent, axis, [(j, j ^ step) for j in range(count)])
        step *= 2
    return flat


def butterfly_gather(flat, axis, steps):
    count = lax.axis_size(axis)
    index = lax.axis_index(axis)
    for step in steps:
        bit = (index // step) % 2
        got = lax.ppermute(flat, axis, [(j, j ^ step) for j in range(count)])
        flat = jnp.where(bit == 1, jnp.concatenate([got, flat]), jnp.concatenate([flat, got]))
    return flat


def descending(count):
    steps = []
    step = count // 2
    while step >= 1:
        steps.append(step)
        step //= 2
    return steps


def quarter_of(space_no, space_count):
    return (space_no % 2) * (space_count // 2) + space_no // 2


def reduce_grads(weight_grad, gain_grad, emb_grad):
    channels = gain_grad.shape[0]
    parts = [weight_grad, emb_grad.reshape(-1, channels), gain_grad[None]]
    rows = sum(part.shape[0] for part in parts)
    devices = lax.axis_size("dx") * lax.axis_size("dy")
    padded_rows = -(-rows // (8 * devices)) * 8 * devices
    parts.append(jnp.zeros((padded_rows - rows, channels), jnp.float32))
    flat = jnp.concatenate(parts, axis=0)
    for axis in ("dx", "dy"):
        flat = butterfly_scatter(flat, axis)
    for axis in ("dy", "dx"):
        flat = butterfly_gather(flat, axis, descending(lax.axis_size(axis)))
    space_count = lax.axis_size("space")
    flat = butterfly_gather(flat, "space", descending(space_count))
    flat = flat.reshape(space_count, padded_rows, channels)
    weight_rows = weight_grad.shape[0]
    emb_rows = emb_grad.size // channels
    conv = flat[:, :weight_rows].reshape(1, 3, 3, channels, channels)
    emb = flat[:, weight_rows : weight_rows + emb_rows].reshape(1, emb_grad.shape[0] * space_count, -1)
    gain = flat[0, weight_rows + emb_rows][None]
    return (conv, gain, emb)


def solution(mesh):
    dp_n = mesh.shape["dp"]
    dx_n = 4 if dp_n % 4 == 0 else 1
    mesh = Mesh(
        mesh.devices.reshape(dp_n // dx_n, dx_n, *mesh.devices.shape[1:]),
        ("dy", "dx", "section", "space"),
    )
    data = ("dy", "dx")
    in_specs = (
        P(data, "space", None, None),
        P(data),
        P(data, "space", None, None),
        P("section", None, None, None, None),
        P("section", None),
        P("section", None, None),
    )
    out_specs = (P("section", None, None, None, None), P("section", None), P("section", None, None))
    return jax.shard_map(
        per_device, mesh=mesh, in_specs=in_specs, out_specs=out_specs, check_vma=False
    )
```

```python
import math

import jax
import jax.numpy as jnp
from jax import lax
from jax.sharding import Mesh, PartitionSpec as P

G = 32
FREQ = 256
MICRO = 2


EPS = 1e-05


def from_behind(value, axis, steps):
    count = lax.axis_size(axis)
    initial, last = (max(0, -steps), min(count, count - steps))
    return lax.ppermute(value, axis, [(source, source + steps) for source in range(initial, last)])


def extended(shard, sides, width):
    for axis, dim in sides:
        size, length = (lax.axis_size(axis), shard.shape[dim])
        up = [(i, (i + 1) % size) for i in range(size - 1)]
        down = [(j, i) for i, j in up]
        last = lax.slice_in_dim(shard, length - width, length, axis=dim)
        initial = lax.slice_in_dim(shard, 0, width, axis=dim)
        before = lax.ppermute(last, axis, up)
        after = lax.ppermute(initial, axis, down)
        shard = jnp.concatenate([before, shard, after], axis=dim)
    return shard


def sinusoid(timesteps, feature_n):
    half_n = feature_n // 2
    freqs = jnp.exp(-math.log(10000.0) * jnp.arange(half_n, dtype=jnp.float32) / half_n)
    angles = timesteps.astype(jnp.float32)[:, None] * freqs[None, :]
    return jnp.concatenate([jnp.cos(angles), jnp.sin(angles)], axis=1)


def group_sums(tensor, groups):
    batch_n, height_n, width_n, channels = tensor.shape
    split = tensor.reshape(batch_n, height_n, width_n, groups, channels // groups)
    return (jnp.sum(split, axis=(1, 2, 4)), jnp.sum(split * split, axis=(1, 2, 4)))


def spread(values, channels):
    return jnp.repeat(values, channels // values.shape[1], axis=1)[:, None, None, :]


def normalize(tensor, first_sum, square_sum, gains, scales, shifts, cell_count):
    channels = tensor.shape[3]
    average = first_sum / cell_count
    inverse = lax.rsqrt(square_sum / cell_count - average * average + EPS)
    normed = (tensor - spread(average, channels)) * spread(inverse, channels) * gains
    return normed * (1.0 + scales[:, None, None, :]) + shifts[:, None, None, :]


def patches(padded, height_n, width_n):
    return jnp.concatenate(
        [
            padded[:, vertical : vertical + height_n, lateral : lateral + width_n, :]
            for vertical in range(3)
            for lateral in range(3)
        ],
        axis=3,
    )


def convolve(padded, matrix):
    batch_n, height_p, width_p, channels = padded.shape
    flat = patches(padded, height_p - 2, width_p - 2).reshape(-1, 9 * channels)
    return jnp.dot(flat, matrix, preferred_element_type=jnp.float32).reshape(
        batch_n, height_p - 2, width_p - 2, matrix.shape[1]
    )


def flip_weight(weight):
    channels = weight.shape[2]
    return jnp.transpose(weight[::-1, ::-1], (0, 1, 3, 2)).reshape(9 * channels, channels)


def silu_slope(pre_act):
    sigmoid_v = jax.nn.sigmoid(pre_act)
    return sigmoid_v * (1.0 + pre_act * (1.0 - sigmoid_v))


def pad_columns(tensor):
    return jnp.pad(tensor, ((0, 0), (0, 0), (1, 1), (0, 0)))


def pick(stacked, index):
    return lax.dynamic_index_in_dim(stacked, index, 0, keepdims=False)


def norm_backward(tensor, first_sum, square_sum, gains, scales, shifts, cell_count, d_pre):

    def mapping(tensor_v, first_v, square_v, gains_v, scales_v, shifts_v):
        return normalize(tensor_v, first_v, square_v, gains_v, scales_v, shifts_v, cell_count)

    _, pull_back = jax.vjp(mapping, tensor, first_sum, square_sum, gains, scales, shifts)
    return pull_back(d_pre)


def pad_both(tensor):
    return jnp.pad(tensor, ((0, 0), (1, 1), (1, 1), (0, 0)))


def block_forward(inputs, flat_weight, gains, scales, shifts, cell_count):
    tensor = inputs.astype(jnp.float32)
    first_sum, square_sum = group_sums(tensor, G)
    pre_act = normalize(tensor, first_sum, square_sum, gains, scales, shifts, cell_count)
    activation = jax.nn.silu(pre_act).astype(jnp.bfloat16)
    padded = pad_both(activation)
    output = (tensor + convolve(padded, flat_weight)).astype(jnp.bfloat16)
    return output, (first_sum, square_sum, padded)


def block_backward(upstream, inputs, saved, flipped, gains, scales, shifts, cell_count):
    first_sum, square_sum, _ = saved
    channels = inputs.shape[3]
    tensor = inputs.astype(jnp.float32)
    pre_act = normalize(tensor, first_sum, square_sum, gains, scales, shifts, cell_count)
    d_act = convolve(pad_both(upstream), flipped)
    d_pre = d_act * silu_slope(pre_act)
    d_tensor, d_first, d_square, d_gains, d_scales, d_shifts = norm_backward(
        tensor, first_sum, square_sum, gains, scales, shifts, cell_count, d_pre
    )
    d_tensor = d_tensor + spread(d_first, channels) + 2.0 * tensor * spread(d_square, channels)
    d_input = (upstream.astype(jnp.float32) + d_tensor).astype(jnp.bfloat16)
    return d_input, (d_gains, d_scales, d_shifts)


def keep(flag, new, old):
    return jax.tree.map(lambda a, b: jnp.where(flag, a, b), new, old)


def per_device(images, steps, out_grad, conv_weight, gn_gain, emb_weight):
    section_count = lax.axis_size("section")
    section_no = lax.axis_index("section")
    space_steps = ascending(lax.axis_size("space"))
    images = butterfly_gather(images, "space", space_steps, dim=1)
    out_grad = butterfly_gather(out_grad, "space", space_steps, dim=1)
    row_count = images.shape[1]
    col_count = images.shape[2]
    channels = images.shape[3]
    cell_count = row_count * col_count * (channels // G)
    weight = conv_weight[0]
    flat_weight = weight.reshape(9 * channels, channels)
    flipped = flip_weight(weight)
    gains = gn_gain[0]
    features = sinusoid(steps, FREQ)
    embedded = jnp.dot(features, emb_weight[0].astype(jnp.float32), precision=lax.Precision.HIGHEST)
    scales = embedded[:, :channels]
    shifts = embedded[:, channels:]
    last = section_count - 1
    carried = images
    kept = None
    for moment in range(section_count):
        inputs = images
        if moment > 0:
            inputs = lax.ppermute(carried, "section", [(moment - 1, moment)])
        if moment == last:
            inputs = (inputs.astype(jnp.float32) + skip.astype(jnp.float32)).astype(jnp.bfloat16)
        output, saved = block_forward(inputs, flat_weight, gains, scales, shifts, cell_count)
        if moment == 0:
            skip = lax.ppermute(output, "section", [(0, last)])
        state = (inputs, saved)
        kept = state if kept is None else keep(section_no == moment, state, kept)
        carried = output
    kept_in, kept_saved = kept
    carried = out_grad
    kept = None
    for moment in range(section_count):
        active = last - moment
        upstream = out_grad
        if moment > 0:
            upstream = lax.ppermute(carried, "section", [(active + 1, active)])
        if active == 0:
            upstream = (upstream.astype(jnp.float32) + skip_grad.astype(jnp.float32)).astype(
                jnp.bfloat16
            )
        d_input, pieces = block_backward(
            upstream, kept_in, kept_saved, flipped, gains, scales, shifts, cell_count
        )
        if moment == 0:
            skip_grad = lax.ppermute(d_input, "section", [(last, 0)])
        state = (upstream, pieces)
        kept = state if kept is None else keep(section_no == active, state, kept)
        carried = d_input
    kept_up, (d_gains, d_scales, d_shifts) = kept
    space_count = lax.axis_size("space")
    space_no = quarter_of(lax.axis_index("space"), space_count)
    patch_rows = 9 * channels // space_count
    flat_patch = patches(kept_saved[2], row_count, col_count).reshape(-1, 9 * channels)
    own_patch = lax.dynamic_slice_in_dim(flat_patch, space_no * patch_rows, patch_rows, axis=1)
    weight_grad = jnp.dot(
        own_patch.T, kept_up.reshape(-1, channels), preferred_element_type=jnp.float32
    )
    emb_rows = FREQ // space_count
    own_features = lax.dynamic_slice_in_dim(features, space_no * emb_rows, emb_rows, axis=1)
    emb_grad = jnp.dot(
        own_features.T,
        jnp.concatenate([d_scales, d_shifts], axis=1),
        precision=lax.Precision.HIGHEST,
    )
    return reduce_grads(weight_grad, d_gains, emb_grad)


def butterfly_scatter(flat, axis):
    count = lax.axis_size(axis)
    index = lax.axis_index(axis)
    step = 1
    while step < count:
        bit = (index // step) % 2
        half = flat.shape[0] // 2
        kept = lax.dynamic_slice_in_dim(flat, bit * half, half, 0)
        sent = lax.dynamic_slice_in_dim(flat, (1 - bit) * half, half, 0)
        flat = kept + lax.ppermute(sent, axis, [(j, j ^ step) for j in range(count)])
        step *= 2
    return flat


def butterfly_gather(flat, axis, steps, dim=0):
    count = lax.axis_size(axis)
    index = lax.axis_index(axis)
    for step in steps:
        bit = (index // step) % 2
        got = lax.ppermute(flat, axis, [(j, j ^ step) for j in range(count)])
        flat = jnp.where(
            bit == 1, jnp.concatenate([got, flat], axis=dim), jnp.concatenate([flat, got], axis=dim)
        )
    return flat


def ascending(count):
    return descending(count)[::-1]


def descending(count):
    steps = []
    step = count // 2
    while step >= 1:
        steps.append(step)
        step //= 2
    return steps


def quarter_of(space_no, space_count):
    return (space_no % 2) * (space_count // 2) + space_no // 2


def reduce_grads(weight_grad, gain_grad, emb_grad):
    channels = gain_grad.shape[0]
    parts = [weight_grad, emb_grad.reshape(-1, channels), gain_grad[None]]
    rows = sum(part.shape[0] for part in parts)
    devices = lax.axis_size("dx") * lax.axis_size("dy")
    padded_rows = -(-rows // (8 * devices)) * 8 * devices
    parts.append(jnp.zeros((padded_rows - rows, channels), jnp.float32))
    flat = jnp.concatenate(parts, axis=0)
    for axis in ("dx", "dy"):
        flat = butterfly_scatter(flat, axis)
    for axis in ("dy", "dx"):
        flat = butterfly_gather(flat, axis, descending(lax.axis_size(axis)))
    space_count = lax.axis_size("space")
    flat = butterfly_gather(flat, "space", descending(space_count))
    flat = flat.reshape(space_count, padded_rows, channels)
    weight_rows = weight_grad.shape[0]
    emb_rows = emb_grad.size // channels
    conv = flat[:, :weight_rows].reshape(1, 3, 3, channels, channels)
    emb = flat[:, weight_rows : weight_rows + emb_rows].reshape(1, emb_grad.shape[0] * space_count, -1)
    gain = flat[0, weight_rows + emb_rows][None]
    return (conv, gain, emb)


def solution(mesh):
    dp_n = mesh.shape["dp"]
    dx_n = 4 if dp_n % 4 == 0 else 1
    mesh = Mesh(
        mesh.devices.reshape(dp_n // dx_n, dx_n, *mesh.devices.shape[1:]),
        ("dy", "dx", "section", "space"),
    )
    data = ("dy", "dx")
    in_specs = (
        P(data, "space", None, None),
        P(data),
        P(data, "space", None, None),
        P("section", None, None, None, None),
        P("section", None),
        P("section", None, None),
    )
    out_specs = (P("section", None, None, None, None), P("section", None), P("section", None, None))
    return jax.shard_map(
        per_device, mesh=mesh, in_specs=in_specs, out_specs=out_specs, check_vma=False
    )
```

```python
import math

import jax
import jax.numpy as jnp
from jax import lax
from jax.sharding import Mesh, PartitionSpec as P

G = 32
FREQ = 256
MICRO = 2


EPS = 1e-05


def from_behind(value, axis, steps):
    count = lax.axis_size(axis)
    initial, last = (max(0, -steps), min(count, count - steps))
    return lax.ppermute(value, axis, [(source, source + steps) for source in range(initial, last)])


def extended(shard, sides, width):
    for axis, dim in sides:
        size, length = (lax.axis_size(axis), shard.shape[dim])
        up = [(i, (i + 1) % size) for i in range(size - 1)]
        down = [(j, i) for i, j in up]
        last = lax.slice_in_dim(shard, length - width, length, axis=dim)
        initial = lax.slice_in_dim(shard, 0, width, axis=dim)
        before = lax.ppermute(last, axis, up)
        after = lax.ppermute(initial, axis, down)
        shard = jnp.concatenate([before, shard, after], axis=dim)
    return shard


def sinusoid(timesteps, feature_n):
    half_n = feature_n // 2
    freqs = jnp.exp(-math.log(10000.0) * jnp.arange(half_n, dtype=jnp.float32) / half_n)
    angles = timesteps.astype(jnp.float32)[:, None] * freqs[None, :]
    return jnp.concatenate([jnp.cos(angles), jnp.sin(angles)], axis=1)


def group_sums(tensor, groups):
    batch_n, height_n, width_n, channels = tensor.shape
    split = tensor.reshape(batch_n, height_n, width_n, groups, channels // groups)
    return (jnp.sum(split, axis=(1, 2, 4)), jnp.sum(split * split, axis=(1, 2, 4)))


def spread(values, channels):
    return jnp.repeat(values, channels // values.shape[1], axis=1)[:, None, None, :]


def normalize(tensor, first_sum, square_sum, gains, scales, shifts, cell_count):
    channels = tensor.shape[3]
    average = first_sum / cell_count
    inverse = lax.rsqrt(square_sum / cell_count - average * average + EPS)
    normed = (tensor - spread(average, channels)) * spread(inverse, channels) * gains
    return normed * (1.0 + scales[:, None, None, :]) + shifts[:, None, None, :]


def patches(padded, height_n, width_n):
    return jnp.concatenate(
        [
            padded[:, vertical : vertical + height_n, lateral : lateral + width_n, :]
            for vertical in range(3)
            for lateral in range(3)
        ],
        axis=3,
    )


def convolve(padded, matrix):
    batch_n, height_p, width_p, channels = padded.shape
    flat = patches(padded, height_p - 2, width_p - 2).reshape(-1, 9 * channels)
    return jnp.dot(flat, matrix, preferred_element_type=jnp.float32).reshape(
        batch_n, height_p - 2, width_p - 2, matrix.shape[1]
    )


def flip_weight(weight):
    channels = weight.shape[2]
    return jnp.transpose(weight[::-1, ::-1], (0, 1, 3, 2)).reshape(9 * channels, channels)


def silu_slope(pre_act):
    sigmoid_v = jax.nn.sigmoid(pre_act)
    return sigmoid_v * (1.0 + pre_act * (1.0 - sigmoid_v))


def pad_columns(tensor):
    return jnp.pad(tensor, ((0, 0), (0, 0), (1, 1), (0, 0)))


def pick(stacked, index):
    return lax.dynamic_index_in_dim(stacked, index, 0, keepdims=False)


def norm_backward(tensor, first_sum, square_sum, gains, scales, shifts, cell_count, d_pre):

    def mapping(tensor_v, first_v, square_v, gains_v, scales_v, shifts_v):
        return normalize(tensor_v, first_v, square_v, gains_v, scales_v, shifts_v, cell_count)

    _, pull_back = jax.vjp(mapping, tensor, first_sum, square_sum, gains, scales, shifts)
    return pull_back(d_pre)


def pad_both(tensor):
    return jnp.pad(tensor, ((0, 0), (1, 1), (1, 1), (0, 0)))


def group_blocks(channels):
    group = jnp.arange(channels) // (channels // G)
    return (group[:, None] == group[None, :]).astype(jnp.float32)


def over_groups(values, blocks):
    return jnp.dot(values, blocks, precision=lax.Precision.HIGHEST)


def normalize_spread(tensor, first_c, square_c, gains, scales, shifts, cell_count):
    average = first_c / cell_count
    inverse = lax.rsqrt(square_c / cell_count - average * average + EPS)
    normed = (tensor - average[:, None, None, :]) * inverse[:, None, None, :] * gains
    return normed * (1.0 + scales[:, None, None, :]) + shifts[:, None, None, :]


def block_forward(inputs, flat_weight, gains, scales, shifts, cell_count):
    tensor = inputs.astype(jnp.float32)
    blocks = group_blocks(tensor.shape[3])
    first_c = over_groups(jnp.sum(tensor, axis=(1, 2)), blocks)
    square_c = over_groups(jnp.sum(tensor * tensor, axis=(1, 2)), blocks)
    pre_act = normalize_spread(tensor, first_c, square_c, gains, scales, shifts, cell_count)
    activation = jax.nn.silu(pre_act).astype(jnp.bfloat16)
    padded = pad_both(activation)
    output = (tensor + convolve(padded, flat_weight)).astype(jnp.bfloat16)
    return output, (first_c, square_c, padded)


def block_backward(upstream, inputs, saved, flipped, gains, scales, shifts, cell_count):
    first_c, square_c, _ = saved
    tensor = inputs.astype(jnp.float32)
    blocks = group_blocks(tensor.shape[3])
    pre_act = normalize_spread(tensor, first_c, square_c, gains, scales, shifts, cell_count)
    d_act = convolve(pad_both(upstream), flipped)
    d_pre = d_act * silu_slope(pre_act)

    def mapping(tensor_v, first_v, square_v, gains_v, scales_v, shifts_v):
        return normalize_spread(tensor_v, first_v, square_v, gains_v, scales_v, shifts_v, cell_count)

    _, pull_back = jax.vjp(mapping, tensor, first_c, square_c, gains, scales, shifts)
    d_tensor, d_first, d_square, d_gains, d_scales, d_shifts = pull_back(d_pre)
    d_first = over_groups(d_first, blocks)[:, None, None, :]
    d_square = over_groups(d_square, blocks)[:, None, None, :]
    d_tensor = d_tensor + d_first + 2.0 * tensor * d_square
    d_input = (upstream.astype(jnp.float32) + d_tensor).astype(jnp.bfloat16)
    return d_input, (d_gains, d_scales, d_shifts)


def keep(flag, new, old):
    return jax.tree.map(lambda a, b: jnp.where(flag, a, b), new, old)


def per_device(images, steps, out_grad, conv_weight, gn_gain, emb_weight):
    section_count = lax.axis_size("section")
    section_no = lax.axis_index("section")
    images = lax.all_gather(images, "space", axis=1, tiled=True)
    out_grad = lax.all_gather(out_grad, "space", axis=1, tiled=True)
    row_count = images.shape[1]
    col_count = images.shape[2]
    channels = images.shape[3]
    cell_count = row_count * col_count * (channels // G)
    weight = conv_weight[0]
    flat_weight = weight.reshape(9 * channels, channels)
    flipped = flip_weight(weight)
    gains = gn_gain[0]
    features = sinusoid(steps, FREQ)
    embedded = jnp.dot(features, emb_weight[0].astype(jnp.float32), precision=lax.Precision.HIGHEST)
    scales = embedded[:, :channels]
    shifts = embedded[:, channels:]
    last = section_count - 1
    carried = images
    kept = None
    for moment in range(section_count):
        inputs = images
        if moment > 0:
            inputs = lax.ppermute(carried, "section", [(moment - 1, moment)])
        if moment == last:
            inputs = (inputs.astype(jnp.float32) + skip.astype(jnp.float32)).astype(jnp.bfloat16)
        output, saved = block_forward(inputs, flat_weight, gains, scales, shifts, cell_count)
        if moment == 0:
            skip = lax.ppermute(output, "section", [(0, last)])
        state = (inputs, saved)
        kept = state if kept is None else keep(section_no == moment, state, kept)
        carried = output
    kept_in, kept_saved = kept
    carried = out_grad
    kept = None
    for moment in range(section_count):
        active = last - moment
        upstream = out_grad
        if moment > 0:
            upstream = lax.ppermute(carried, "section", [(active + 1, active)])
        if active == 0:
            upstream = (upstream.astype(jnp.float32) + skip_grad.astype(jnp.float32)).astype(
                jnp.bfloat16
            )
        d_input, pieces = block_backward(
            upstream, kept_in, kept_saved, flipped, gains, scales, shifts, cell_count
        )
        if moment == 0:
            skip_grad = lax.ppermute(d_input, "section", [(last, 0)])
        state = (upstream, pieces)
        kept = state if kept is None else keep(section_no == active, state, kept)
        carried = d_input
    kept_up, (d_gains, d_scales, d_shifts) = kept
    space_count = lax.axis_size("space")
    space_no = quarter_of(lax.axis_index("space"), space_count)
    patch_rows = 9 * channels // space_count
    flat_patch = patches(kept_saved[2], row_count, col_count).reshape(-1, 9 * channels)
    own_patch = lax.dynamic_slice_in_dim(flat_patch, space_no * patch_rows, patch_rows, axis=1)
    weight_grad = jnp.dot(
        own_patch.T, kept_up.reshape(-1, channels), preferred_element_type=jnp.float32
    )
    emb_rows = FREQ // space_count
    own_features = lax.dynamic_slice_in_dim(features, space_no * emb_rows, emb_rows, axis=1)
    emb_grad = jnp.dot(
        own_features.T,
        jnp.concatenate([d_scales, d_shifts], axis=1),
        precision=lax.Precision.HIGHEST,
    )
    return reduce_grads(weight_grad, d_gains, emb_grad)


def butterfly_scatter(flat, axis):
    count = lax.axis_size(axis)
    index = lax.axis_index(axis)
    step = 1
    while step < count:
        bit = (index // step) % 2
        half = flat.shape[0] // 2
        kept = lax.dynamic_slice_in_dim(flat, bit * half, half, 0)
        sent = lax.dynamic_slice_in_dim(flat, (1 - bit) * half, half, 0)
        flat = kept + lax.ppermute(sent, axis, [(j, j ^ step) for j in range(count)])
        step *= 2
    return flat


def butterfly_gather(flat, axis, steps):
    count = lax.axis_size(axis)
    index = lax.axis_index(axis)
    for step in steps:
        bit = (index // step) % 2
        got = lax.ppermute(flat, axis, [(j, j ^ step) for j in range(count)])
        flat = jnp.where(bit == 1, jnp.concatenate([got, flat]), jnp.concatenate([flat, got]))
    return flat


def descending(count):
    steps = []
    step = count // 2
    while step >= 1:
        steps.append(step)
        step //= 2
    return steps


def quarter_of(space_no, space_count):
    return (space_no % 2) * (space_count // 2) + space_no // 2


def reduce_grads(weight_grad, gain_grad, emb_grad):
    channels = gain_grad.shape[0]
    parts = [weight_grad, emb_grad.reshape(-1, channels), gain_grad[None]]
    rows = sum(part.shape[0] for part in parts)
    devices = lax.axis_size("dx") * lax.axis_size("dy")
    padded_rows = -(-rows // (8 * devices)) * 8 * devices
    parts.append(jnp.zeros((padded_rows - rows, channels), jnp.float32))
    flat = jnp.concatenate(parts, axis=0)
    for axis in ("dx", "dy"):
        flat = butterfly_scatter(flat, axis)
    for axis in ("dy", "dx"):
        flat = butterfly_gather(flat, axis, descending(lax.axis_size(axis)))
    space_count = lax.axis_size("space")
    flat = butterfly_gather(flat, "space", descending(space_count))
    flat = flat.reshape(space_count, padded_rows, channels)
    weight_rows = weight_grad.shape[0]
    emb_rows = emb_grad.size // channels
    conv = flat[:, :weight_rows].reshape(1, 3, 3, channels, channels)
    emb = flat[:, weight_rows : weight_rows + emb_rows].reshape(1, emb_grad.shape[0] * space_count, -1)
    gain = flat[0, weight_rows + emb_rows][None]
    return (conv, gain, emb)


def solution(mesh):
    dp_n = mesh.shape["dp"]
    dx_n = 4 if dp_n % 4 == 0 else 1
    mesh = Mesh(
        mesh.devices.reshape(dp_n // dx_n, dx_n, *mesh.devices.shape[1:]),
        ("dy", "dx", "section", "space"),
    )
    data = ("dy", "dx")
    in_specs = (
        P(data, "space", None, None),
        P(data),
        P(data, "space", None, None),
        P("section", None, None, None, None),
        P("section", None),
        P("section", None, None),
    )
    out_specs = (P("section", None, None, None, None), P("section", None), P("section", None, None))
    return jax.shard_map(
        per_device, mesh=mesh, in_specs=in_specs, out_specs=out_specs, check_vma=False
    )
```

```python
import math

import jax
import jax.numpy as jnp
from jax import lax
from jax.sharding import Mesh, PartitionSpec as P

G = 32
FREQ = 256
MICRO = 2


EPS = 1e-05


def from_behind(value, axis, steps):
    count = lax.axis_size(axis)
    initial, last = (max(0, -steps), min(count, count - steps))
    return lax.ppermute(value, axis, [(source, source + steps) for source in range(initial, last)])


def extended(shard, sides, width):
    for axis, dim in sides:
        size, length = (lax.axis_size(axis), shard.shape[dim])
        up = [(i, (i + 1) % size) for i in range(size - 1)]
        down = [(j, i) for i, j in up]
        last = lax.slice_in_dim(shard, length - width, length, axis=dim)
        initial = lax.slice_in_dim(shard, 0, width, axis=dim)
        before = lax.ppermute(last, axis, up)
        after = lax.ppermute(initial, axis, down)
        shard = jnp.concatenate([before, shard, after], axis=dim)
    return shard


def sinusoid(timesteps, feature_n):
    half_n = feature_n // 2
    freqs = jnp.exp(-math.log(10000.0) * jnp.arange(half_n, dtype=jnp.float32) / half_n)
    angles = timesteps.astype(jnp.float32)[:, None] * freqs[None, :]
    return jnp.concatenate([jnp.cos(angles), jnp.sin(angles)], axis=1)


def group_sums(tensor, groups):
    batch_n, height_n, width_n, channels = tensor.shape
    split = tensor.reshape(batch_n, height_n, width_n, groups, channels // groups)
    return (jnp.sum(split, axis=(1, 2, 4)), jnp.sum(split * split, axis=(1, 2, 4)))


def spread(values, channels):
    return jnp.repeat(values, channels // values.shape[1], axis=1)[:, None, None, :]


def normalize(tensor, first_sum, square_sum, gains, scales, shifts, cell_count):
    channels = tensor.shape[3]
    average = first_sum / cell_count
    inverse = lax.rsqrt(square_sum / cell_count - average * average + EPS)
    normed = (tensor - spread(average, channels)) * spread(inverse, channels) * gains
    return normed * (1.0 + scales[:, None, None, :]) + shifts[:, None, None, :]


def patches(padded, height_n, width_n):
    return jnp.concatenate(
        [
            padded[:, vertical : vertical + height_n, lateral : lateral + width_n, :]
            for vertical in range(3)
            for lateral in range(3)
        ],
        axis=3,
    )


def convolve(padded, matrix):
    batch_n, height_p, width_p, channels = padded.shape
    flat = patches(padded, height_p - 2, width_p - 2).reshape(-1, 9 * channels)
    return jnp.dot(flat, matrix, preferred_element_type=jnp.float32).reshape(
        batch_n, height_p - 2, width_p - 2, matrix.shape[1]
    )


def flip_weight(weight):
    channels = weight.shape[2]
    return jnp.transpose(weight[::-1, ::-1], (0, 1, 3, 2)).reshape(9 * channels, channels)


def silu_slope(pre_act):
    sigmoid_v = jax.nn.sigmoid(pre_act)
    return sigmoid_v * (1.0 + pre_act * (1.0 - sigmoid_v))


def pad_columns(tensor):
    return jnp.pad(tensor, ((0, 0), (0, 0), (1, 1), (0, 0)))


def pick(stacked, index):
    return lax.dynamic_index_in_dim(stacked, index, 0, keepdims=False)


def norm_backward(tensor, first_sum, square_sum, gains, scales, shifts, cell_count, d_pre):

    def mapping(tensor_v, first_v, square_v, gains_v, scales_v, shifts_v):
        return normalize(tensor_v, first_v, square_v, gains_v, scales_v, shifts_v, cell_count)

    _, pull_back = jax.vjp(mapping, tensor, first_sum, square_sum, gains, scales, shifts)
    return pull_back(d_pre)


def pad_both(tensor):
    return jnp.pad(tensor, ((0, 0), (1, 1), (1, 1), (0, 0)))


def group_blocks(channels):
    group = jnp.arange(channels) // (channels // G)
    return (group[:, None] == group[None, :]).astype(jnp.float32)


def over_groups(values, blocks):
    return jnp.dot(values, blocks, precision=lax.Precision.HIGHEST)


def normalize_spread(tensor, first_c, square_c, gains, scales, shifts, cell_count):
    average = first_c / cell_count
    inverse = lax.rsqrt(square_c / cell_count - average * average + EPS)
    normed = (tensor - average[:, None, None, :]) * inverse[:, None, None, :] * gains
    return normed * (1.0 + scales[:, None, None, :]) + shifts[:, None, None, :]


def block_forward(inputs, flat_weight, gains, scales, shifts, cell_count):
    tensor = inputs.astype(jnp.float32)
    blocks = group_blocks(tensor.shape[3])
    first_c = over_groups(jnp.sum(tensor, axis=(1, 2)), blocks)
    square_c = over_groups(jnp.sum(tensor * tensor, axis=(1, 2)), blocks)
    pre_act = normalize_spread(tensor, first_c, square_c, gains, scales, shifts, cell_count)
    activation = jax.nn.silu(pre_act).astype(jnp.bfloat16)
    padded = pad_both(activation)
    output = (tensor + convolve(padded, flat_weight)).astype(jnp.bfloat16)
    return output, (first_c, square_c, padded)


def block_backward(upstream, inputs, saved, flipped, gains, scales, shifts, cell_count):
    first_c, square_c, _ = saved
    tensor = inputs.astype(jnp.float32)
    blocks = group_blocks(tensor.shape[3])
    pre_act = normalize_spread(tensor, first_c, square_c, gains, scales, shifts, cell_count)
    d_act = convolve(pad_both(upstream), flipped)
    d_pre = d_act * silu_slope(pre_act)

    def mapping(tensor_v, first_v, square_v, gains_v, scales_v, shifts_v):
        return normalize_spread(tensor_v, first_v, square_v, gains_v, scales_v, shifts_v, cell_count)

    _, pull_back = jax.vjp(mapping, tensor, first_c, square_c, gains, scales, shifts)
    d_tensor, d_first, d_square, d_gains, d_scales, d_shifts = pull_back(d_pre)
    d_first = over_groups(d_first, blocks)[:, None, None, :]
    d_square = over_groups(d_square, blocks)[:, None, None, :]
    d_tensor = d_tensor + d_first + 2.0 * tensor * d_square
    d_input = (upstream.astype(jnp.float32) + d_tensor).astype(jnp.bfloat16)
    return d_input, (d_gains, d_scales, d_shifts)


def keep(flag, new, old):
    return jax.tree.map(lambda a, b: jnp.where(flag, a, b), new, old)


def per_device(images, steps, out_grad, conv_weight, gn_gain, emb_weight):
    section_count = lax.axis_size("section")
    section_no = lax.axis_index("section")
    both = lax.all_gather(jnp.stack([images, out_grad]), "space", axis=2, tiled=True)
    images = both[0]
    out_grad = both[1]
    row_count = images.shape[1]
    col_count = images.shape[2]
    channels = images.shape[3]
    cell_count = row_count * col_count * (channels // G)
    weight = conv_weight[0]
    flat_weight = weight.reshape(9 * channels, channels)
    flipped = flip_weight(weight)
    gains = gn_gain[0]
    features = sinusoid(steps, FREQ)
    embedded = jnp.dot(features, emb_weight[0].astype(jnp.float32), precision=lax.Precision.HIGHEST)
    scales = embedded[:, :channels]
    shifts = embedded[:, channels:]
    last = section_count - 1
    carried = images
    kept = None
    for moment in range(section_count):
        inputs = images
        if moment > 0:
            inputs = lax.ppermute(carried, "section", [(moment - 1, moment)])
        if moment == last:
            inputs = (inputs.astype(jnp.float32) + skip.astype(jnp.float32)).astype(jnp.bfloat16)
        output, saved = block_forward(inputs, flat_weight, gains, scales, shifts, cell_count)
        if moment == 0:
            skip = lax.ppermute(output, "section", [(0, last)])
        state = (inputs, saved)
        kept = state if kept is None else keep(section_no == moment, state, kept)
        carried = output
    kept_in, kept_saved = kept
    carried = out_grad
    kept = None
    for moment in range(section_count):
        active = last - moment
        upstream = out_grad
        if moment > 0:
            upstream = lax.ppermute(carried, "section", [(active + 1, active)])
        if active == 0:
            upstream = (upstream.astype(jnp.float32) + skip_grad.astype(jnp.float32)).astype(
                jnp.bfloat16
            )
        d_input, pieces = block_backward(
            upstream, kept_in, kept_saved, flipped, gains, scales, shifts, cell_count
        )
        if moment == 0:
            skip_grad = lax.ppermute(d_input, "section", [(last, 0)])
        state = (upstream, pieces)
        kept = state if kept is None else keep(section_no == active, state, kept)
        carried = d_input
    kept_up, (d_gains, d_scales, d_shifts) = kept
    space_count = lax.axis_size("space")
    space_no = quarter_of(lax.axis_index("space"), space_count)
    patch_rows = 9 * channels // space_count
    flat_patch = patches(kept_saved[2], row_count, col_count).reshape(-1, 9 * channels)
    own_patch = lax.dynamic_slice_in_dim(flat_patch, space_no * patch_rows, patch_rows, axis=1)
    weight_grad = jnp.dot(
        own_patch.T, kept_up.reshape(-1, channels), preferred_element_type=jnp.float32
    )
    emb_rows = FREQ // space_count
    own_features = lax.dynamic_slice_in_dim(features, space_no * emb_rows, emb_rows, axis=1)
    emb_grad = jnp.dot(
        own_features.T,
        jnp.concatenate([d_scales, d_shifts], axis=1),
        precision=lax.Precision.HIGHEST,
    )
    return reduce_grads(weight_grad, d_gains, emb_grad)


def butterfly_scatter(flat, axis):
    count = lax.axis_size(axis)
    index = lax.axis_index(axis)
    step = 1
    while step < count:
        bit = (index // step) % 2
        half = flat.shape[0] // 2
        kept = lax.dynamic_slice_in_dim(flat, bit * half, half, 0)
        sent = lax.dynamic_slice_in_dim(flat, (1 - bit) * half, half, 0)
        flat = kept + lax.ppermute(sent, axis, [(j, j ^ step) for j in range(count)])
        step *= 2
    return flat


def butterfly_gather(flat, axis, steps):
    count = lax.axis_size(axis)
    index = lax.axis_index(axis)
    for step in steps:
        bit = (index // step) % 2
        got = lax.ppermute(flat, axis, [(j, j ^ step) for j in range(count)])
        flat = jnp.where(bit == 1, jnp.concatenate([got, flat]), jnp.concatenate([flat, got]))
    return flat


def descending(count):
    steps = []
    step = count // 2
    while step >= 1:
        steps.append(step)
        step //= 2
    return steps


def quarter_of(space_no, space_count):
    return (space_no % 2) * (space_count // 2) + space_no // 2


def reduce_grads(weight_grad, gain_grad, emb_grad):
    channels = gain_grad.shape[0]
    parts = [weight_grad, emb_grad.reshape(-1, channels), gain_grad[None]]
    rows = sum(part.shape[0] for part in parts)
    devices = lax.axis_size("dx") * lax.axis_size("dy")
    padded_rows = -(-rows // (8 * devices)) * 8 * devices
    parts.append(jnp.zeros((padded_rows - rows, channels), jnp.float32))
    flat = jnp.concatenate(parts, axis=0)
    for axis in ("dx", "dy"):
        flat = butterfly_scatter(flat, axis)
    for axis in ("dy", "dx"):
        flat = butterfly_gather(flat, axis, descending(lax.axis_size(axis)))
    space_count = lax.axis_size("space")
    flat = butterfly_gather(flat, "space", descending(space_count))
    flat = flat.reshape(space_count, padded_rows, channels)
    weight_rows = weight_grad.shape[0]
    emb_rows = emb_grad.size // channels
    conv = flat[:, :weight_rows].reshape(1, 3, 3, channels, channels)
    emb = flat[:, weight_rows : weight_rows + emb_rows].reshape(1, emb_grad.shape[0] * space_count, -1)
    gain = flat[0, weight_rows + emb_rows][None]
    return (conv, gain, emb)


def solution(mesh):
    dp_n = mesh.shape["dp"]
    dx_n = 4 if dp_n % 4 == 0 else 1
    mesh = Mesh(
        mesh.devices.reshape(dp_n // dx_n, dx_n, *mesh.devices.shape[1:]),
        ("dy", "dx", "section", "space"),
    )
    data = ("dy", "dx")
    in_specs = (
        P(data, "space", None, None),
        P(data),
        P(data, "space", None, None),
        P("section", None, None, None, None),
        P("section", None),
        P("section", None, None),
    )
    out_specs = (P("section", None, None, None, None), P("section", None), P("section", None, None))
    return jax.shard_map(
        per_device, mesh=mesh, in_specs=in_specs, out_specs=out_specs, check_vma=False
    )
```

```python
import math

import jax
import jax.numpy as jnp
from jax import lax
from jax.sharding import Mesh, PartitionSpec as P

G = 32
FREQ = 256
MICRO = 2


EPS = 1e-05


def from_behind(value, axis, steps):
    count = lax.axis_size(axis)
    initial, last = (max(0, -steps), min(count, count - steps))
    return lax.ppermute(value, axis, [(source, source + steps) for source in range(initial, last)])


def extended(shard, sides, width):
    for axis, dim in sides:
        size, length = (lax.axis_size(axis), shard.shape[dim])
        up = [(i, (i + 1) % size) for i in range(size - 1)]
        down = [(j, i) for i, j in up]
        last = lax.slice_in_dim(shard, length - width, length, axis=dim)
        initial = lax.slice_in_dim(shard, 0, width, axis=dim)
        before = lax.ppermute(last, axis, up)
        after = lax.ppermute(initial, axis, down)
        shard = jnp.concatenate([before, shard, after], axis=dim)
    return shard


def sinusoid(timesteps, feature_n):
    half_n = feature_n // 2
    freqs = jnp.exp(-math.log(10000.0) * jnp.arange(half_n, dtype=jnp.float32) / half_n)
    angles = timesteps.astype(jnp.float32)[:, None] * freqs[None, :]
    return jnp.concatenate([jnp.cos(angles), jnp.sin(angles)], axis=1)


def group_sums(tensor, groups):
    batch_n, height_n, width_n, channels = tensor.shape
    split = tensor.reshape(batch_n, height_n, width_n, groups, channels // groups)
    return (jnp.sum(split, axis=(1, 2, 4)), jnp.sum(split * split, axis=(1, 2, 4)))


def spread(values, channels):
    return jnp.repeat(values, channels // values.shape[1], axis=1)[:, None, None, :]


def normalize(tensor, first_sum, square_sum, gains, scales, shifts, cell_count):
    channels = tensor.shape[3]
    average = first_sum / cell_count
    inverse = lax.rsqrt(square_sum / cell_count - average * average + EPS)
    normed = (tensor - spread(average, channels)) * spread(inverse, channels) * gains
    return normed * (1.0 + scales[:, None, None, :]) + shifts[:, None, None, :]


def patches(padded, height_n, width_n):
    return jnp.concatenate(
        [
            padded[:, vertical : vertical + height_n, lateral : lateral + width_n, :]
            for vertical in range(3)
            for lateral in range(3)
        ],
        axis=3,
    )


def convolve(padded, matrix):
    batch_n, height_p, width_p, channels = padded.shape
    flat = patches(padded, height_p - 2, width_p - 2).reshape(-1, 9 * channels)
    return jnp.dot(flat, matrix, preferred_element_type=jnp.float32).reshape(
        batch_n, height_p - 2, width_p - 2, matrix.shape[1]
    )


def flip_weight(weight):
    channels = weight.shape[2]
    return jnp.transpose(weight[::-1, ::-1], (0, 1, 3, 2)).reshape(9 * channels, channels)


def silu_slope(pre_act):
    sigmoid_v = jax.nn.sigmoid(pre_act)
    return sigmoid_v * (1.0 + pre_act * (1.0 - sigmoid_v))


def pad_columns(tensor):
    return jnp.pad(tensor, ((0, 0), (0, 0), (1, 1), (0, 0)))


def pick(stacked, index):
    return lax.dynamic_index_in_dim(stacked, index, 0, keepdims=False)


def norm_backward(tensor, first_sum, square_sum, gains, scales, shifts, cell_count, d_pre):

    def mapping(tensor_v, first_v, square_v, gains_v, scales_v, shifts_v):
        return normalize(tensor_v, first_v, square_v, gains_v, scales_v, shifts_v, cell_count)

    _, pull_back = jax.vjp(mapping, tensor, first_sum, square_sum, gains, scales, shifts)
    return pull_back(d_pre)


def pad_both(tensor):
    return jnp.pad(tensor, ((0, 0), (1, 1), (1, 1), (0, 0)))


def group_blocks(channels):
    group = jnp.arange(channels) // (channels // G)
    return (group[:, None] == group[None, :]).astype(jnp.float32)


def over_groups(values, blocks):
    return jnp.dot(values, blocks, precision=lax.Precision.HIGHEST)


def normalize_spread(tensor, first_c, square_c, gains, scales, shifts, cell_count):
    average = first_c / cell_count
    inverse = lax.rsqrt(square_c / cell_count - average * average + EPS)
    normed = (tensor - average[:, None, None, :]) * inverse[:, None, None, :] * gains
    return normed * (1.0 + scales[:, None, None, :]) + shifts[:, None, None, :]


def block_forward(inputs, flat_weight, gains, scales, shifts, cell_count):
    tensor = inputs.astype(jnp.float32)
    blocks = group_blocks(tensor.shape[3])
    first_c = over_groups(jnp.sum(tensor, axis=(1, 2)), blocks)
    square_c = over_groups(jnp.sum(tensor * tensor, axis=(1, 2)), blocks)
    pre_act = normalize_spread(tensor, first_c, square_c, gains, scales, shifts, cell_count)
    activation = jax.nn.silu(pre_act).astype(jnp.bfloat16)
    padded = pad_both(activation)
    output = (tensor + convolve(padded, flat_weight)).astype(jnp.bfloat16)
    return output, (first_c, square_c, padded)


def block_backward(upstream, inputs, saved, flipped, gains, scales, shifts, cell_count):
    first_c, square_c, _ = saved
    tensor = inputs.astype(jnp.float32)
    blocks = group_blocks(tensor.shape[3])
    pre_act = normalize_spread(tensor, first_c, square_c, gains, scales, shifts, cell_count)
    d_act = convolve(pad_both(upstream), flipped)
    d_pre = d_act * silu_slope(pre_act)

    def mapping(tensor_v, first_v, square_v, gains_v, scales_v, shifts_v):
        return normalize_spread(tensor_v, first_v, square_v, gains_v, scales_v, shifts_v, cell_count)

    _, pull_back = jax.vjp(mapping, tensor, first_c, square_c, gains, scales, shifts)
    d_tensor, d_first, d_square, d_gains, d_scales, d_shifts = pull_back(d_pre)
    d_first = over_groups(d_first, blocks)[:, None, None, :]
    d_square = over_groups(d_square, blocks)[:, None, None, :]
    d_tensor = d_tensor + d_first + 2.0 * tensor * d_square
    d_input = (upstream.astype(jnp.float32) + d_tensor).astype(jnp.bfloat16)
    return d_input, (d_gains, d_scales, d_shifts)


def keep(flag, new, old):
    return jax.tree.map(lambda a, b: jnp.where(flag, a, b), new, old)


def per_device(images, steps, out_grad, conv_weight, gn_gain, emb_weight):
    section_count = lax.axis_size("section")
    section_no = lax.axis_index("section")
    images = lax.all_gather(images, "space", axis=1, tiled=True)
    out_grad = lax.all_gather(out_grad, "space", axis=1, tiled=True)
    row_count = images.shape[1]
    col_count = images.shape[2]
    channels = images.shape[3]
    cell_count = row_count * col_count * (channels // G)
    weight = conv_weight[0]
    flat_weight = weight.reshape(9 * channels, channels)
    flipped = flip_weight(weight)
    gains = gn_gain[0]
    features = sinusoid(steps, FREQ)
    embedded = jnp.dot(features, emb_weight[0].astype(jnp.float32), precision=lax.Precision.HIGHEST)
    scales = embedded[:, :channels]
    shifts = embedded[:, channels:]
    last = section_count - 1
    carried = images
    kept = None
    for moment in range(section_count):
        inputs = images
        if moment > 0:
            inputs = lax.ppermute(carried, "section", [(moment - 1, moment)])
        if moment == last:
            inputs = (inputs.astype(jnp.float32) + skip.astype(jnp.float32)).astype(jnp.bfloat16)
        output, saved = block_forward(inputs, flat_weight, gains, scales, shifts, cell_count)
        if moment == 0:
            skip = lax.ppermute(output, "section", [(0, last)])
        state = (inputs, saved)
        kept = state if kept is None else keep(section_no == moment, state, kept)
        carried = output
    kept_in, kept_saved = kept
    carried = out_grad
    kept = None
    for moment in range(section_count):
        active = last - moment
        upstream = out_grad
        if moment > 0:
            upstream = lax.ppermute(carried, "section", [(active + 1, active)])
        if active == 0:
            upstream = (upstream.astype(jnp.float32) + skip_grad.astype(jnp.float32)).astype(
                jnp.bfloat16
            )
        d_input, pieces = block_backward(
            upstream, kept_in, kept_saved, flipped, gains, scales, shifts, cell_count
        )
        if moment == 0:
            skip_grad = lax.ppermute(d_input, "section", [(last, 0)])
        state = (upstream, pieces)
        kept = state if kept is None else keep(section_no == active, state, kept)
        carried = d_input
    kept_up, (d_gains, d_scales, d_shifts) = kept
    space_count = lax.axis_size("space")
    space_no = quarter_of(lax.axis_index("space"), space_count)
    patch_rows = 9 * channels // space_count
    flat_patch = patches(kept_saved[2], row_count, col_count).reshape(-1, 9 * channels)
    own_patch = lax.dynamic_slice_in_dim(flat_patch, space_no * patch_rows, patch_rows, axis=1)
    weight_grad = jnp.dot(
        own_patch.T, kept_up.reshape(-1, channels), preferred_element_type=jnp.float32
    )
    emb_rows = FREQ // space_count
    own_features = lax.dynamic_slice_in_dim(features, space_no * emb_rows, emb_rows, axis=1)
    emb_grad = jnp.dot(
        own_features.T,
        jnp.concatenate([d_scales, d_shifts], axis=1),
        precision=lax.Precision.HIGHEST,
    )
    return reduce_grads(weight_grad, d_gains, emb_grad)


def butterfly_scatter(flat, axis):
    count = lax.axis_size(axis)
    index = lax.axis_index(axis)
    step = 1
    while step < count:
        bit = (index // step) % 2
        half = flat.shape[0] // 2
        kept = lax.dynamic_slice_in_dim(flat, bit * half, half, 0)
        sent = lax.dynamic_slice_in_dim(flat, (1 - bit) * half, half, 0)
        flat = kept + lax.ppermute(sent, axis, [(j, j ^ step) for j in range(count)])
        step *= 2
    return flat


def butterfly_gather(flat, axis, steps):
    count = lax.axis_size(axis)
    index = lax.axis_index(axis)
    for step in steps:
        bit = (index // step) % 2
        got = lax.ppermute(flat, axis, [(j, j ^ step) for j in range(count)])
        flat = jnp.where(bit == 1, jnp.concatenate([got, flat]), jnp.concatenate([flat, got]))
    return flat


def descending(count):
    steps = []
    step = count // 2
    while step >= 1:
        steps.append(step)
        step //= 2
    return steps


def quarter_of(space_no, space_count):
    return (space_no % 2) * (space_count // 2) + space_no // 2


def reduce_grads(weight_grad, gain_grad, emb_grad):
    channels = gain_grad.shape[0]
    parts = [weight_grad, emb_grad.reshape(-1, channels), gain_grad[None]]
    rows = sum(part.shape[0] for part in parts)
    devices = lax.axis_size("dx") * lax.axis_size("dy")
    padded_rows = -(-rows // (8 * devices)) * 8 * devices
    parts.append(jnp.zeros((padded_rows - rows, channels), jnp.float32))
    flat = jnp.concatenate(parts, axis=0)
    for axis in ("dx", "dy"):
        flat = butterfly_scatter(flat, axis)
    flat = flat.astype(jnp.bfloat16)
    for axis in ("dy", "dx"):
        flat = butterfly_gather(flat, axis, descending(lax.axis_size(axis)))
    space_count = lax.axis_size("space")
    flat = butterfly_gather(flat, "space", descending(space_count))
    flat = flat.reshape(space_count, padded_rows, channels).astype(jnp.float32)
    weight_rows = weight_grad.shape[0]
    emb_rows = emb_grad.size // channels
    conv = flat[:, :weight_rows].reshape(1, 3, 3, channels, channels)
    emb = flat[:, weight_rows : weight_rows + emb_rows].reshape(1, emb_grad.shape[0] * space_count, -1)
    gain = flat[0, weight_rows + emb_rows][None]
    return (conv, gain, emb)


def solution(mesh):
    dp_n = mesh.shape["dp"]
    dx_n = 4 if dp_n % 4 == 0 else 1
    mesh = Mesh(
        mesh.devices.reshape(dp_n // dx_n, dx_n, *mesh.devices.shape[1:]),
        ("dy", "dx", "section", "space"),
    )
    data = ("dy", "dx")
    in_specs = (
        P(data, "space", None, None),
        P(data),
        P(data, "space", None, None),
        P("section", None, None, None, None),
        P("section", None),
        P("section", None, None),
    )
    out_specs = (P("section", None, None, None, None), P("section", None), P("section", None, None))
    return jax.shard_map(
        per_device, mesh=mesh, in_specs=in_specs, out_specs=out_specs, check_vma=False
    )
```

```python
import math

import jax
import jax.numpy as jnp
from jax import lax
from jax.sharding import Mesh, PartitionSpec as P

G = 32
FREQ = 256
MICRO = 2


EPS = 1e-05


def from_behind(value, axis, steps):
    count = lax.axis_size(axis)
    initial, last = (max(0, -steps), min(count, count - steps))
    return lax.ppermute(value, axis, [(source, source + steps) for source in range(initial, last)])


def extended(shard, sides, width):
    for axis, dim in sides:
        size, length = (lax.axis_size(axis), shard.shape[dim])
        up = [(i, (i + 1) % size) for i in range(size - 1)]
        down = [(j, i) for i, j in up]
        last = lax.slice_in_dim(shard, length - width, length, axis=dim)
        initial = lax.slice_in_dim(shard, 0, width, axis=dim)
        before = lax.ppermute(last, axis, up)
        after = lax.ppermute(initial, axis, down)
        shard = jnp.concatenate([before, shard, after], axis=dim)
    return shard


def sinusoid(timesteps, feature_n):
    half_n = feature_n // 2
    freqs = jnp.exp(-math.log(10000.0) * jnp.arange(half_n, dtype=jnp.float32) / half_n)
    angles = timesteps.astype(jnp.float32)[:, None] * freqs[None, :]
    return jnp.concatenate([jnp.cos(angles), jnp.sin(angles)], axis=1)


def group_sums(tensor, groups):
    batch_n, height_n, width_n, channels = tensor.shape
    split = tensor.reshape(batch_n, height_n, width_n, groups, channels // groups)
    return (jnp.sum(split, axis=(1, 2, 4)), jnp.sum(split * split, axis=(1, 2, 4)))


def spread(values, channels):
    return jnp.repeat(values, channels // values.shape[1], axis=1)[:, None, None, :]


def normalize(tensor, first_sum, square_sum, gains, scales, shifts, cell_count):
    channels = tensor.shape[3]
    average = first_sum / cell_count
    inverse = lax.rsqrt(square_sum / cell_count - average * average + EPS)
    normed = (tensor - spread(average, channels)) * spread(inverse, channels) * gains
    return normed * (1.0 + scales[:, None, None, :]) + shifts[:, None, None, :]


def patches(padded, height_n, width_n):
    return jnp.concatenate(
        [
            padded[:, vertical : vertical + height_n, lateral : lateral + width_n, :]
            for vertical in range(3)
            for lateral in range(3)
        ],
        axis=3,
    )


def convolve(padded, matrix):
    batch_n, height_p, width_p, channels = padded.shape
    flat = patches(padded, height_p - 2, width_p - 2).reshape(-1, 9 * channels)
    return jnp.dot(flat, matrix, preferred_element_type=jnp.float32).reshape(
        batch_n, height_p - 2, width_p - 2, matrix.shape[1]
    )


def flip_weight(weight):
    channels = weight.shape[2]
    return jnp.transpose(weight[::-1, ::-1], (0, 1, 3, 2)).reshape(9 * channels, channels)


def silu_slope(pre_act):
    sigmoid_v = jax.nn.sigmoid(pre_act)
    return sigmoid_v * (1.0 + pre_act * (1.0 - sigmoid_v))


def pad_columns(tensor):
    return jnp.pad(tensor, ((0, 0), (0, 0), (1, 1), (0, 0)))


def pick(stacked, index):
    return lax.dynamic_index_in_dim(stacked, index, 0, keepdims=False)


def norm_backward(tensor, first_sum, square_sum, gains, scales, shifts, cell_count, d_pre):

    def mapping(tensor_v, first_v, square_v, gains_v, scales_v, shifts_v):
        return normalize(tensor_v, first_v, square_v, gains_v, scales_v, shifts_v, cell_count)

    _, pull_back = jax.vjp(mapping, tensor, first_sum, square_sum, gains, scales, shifts)
    return pull_back(d_pre)


def pad_both(tensor):
    return jnp.pad(tensor, ((0, 0), (1, 1), (1, 1), (0, 0)))


def group_blocks(channels):
    group = jnp.arange(channels) // (channels // G)
    return (group[:, None] == group[None, :]).astype(jnp.float32)


def over_groups(values, blocks):
    return jnp.dot(values, blocks, precision=lax.Precision.HIGHEST)


def normalize_spread(tensor, first_c, square_c, gains, scales, shifts, cell_count):
    average = first_c / cell_count
    inverse = lax.rsqrt(square_c / cell_count - average * average + EPS)
    normed = (tensor - average[:, None, None, :]) * inverse[:, None, None, :] * gains
    return normed * (1.0 + scales[:, None, None, :]) + shifts[:, None, None, :]


def block_forward(inputs, flat_weight, gains, scales, shifts, cell_count):
    tensor = inputs.astype(jnp.float32)
    blocks = group_blocks(tensor.shape[3])
    first_c = over_groups(jnp.sum(tensor, axis=(1, 2)), blocks)
    square_c = over_groups(jnp.sum(tensor * tensor, axis=(1, 2)), blocks)
    pre_act = normalize_spread(tensor, first_c, square_c, gains, scales, shifts, cell_count)
    activation = jax.nn.silu(pre_act).astype(jnp.bfloat16)
    padded = pad_both(activation)
    output = (tensor + convolve(padded, flat_weight)).astype(jnp.bfloat16)
    return output, (first_c, square_c, padded)


def block_backward(upstream, inputs, saved, flipped, gains, scales, shifts, cell_count):
    first_c, square_c, _ = saved
    tensor = inputs.astype(jnp.float32)
    blocks = group_blocks(tensor.shape[3])
    pre_act = normalize_spread(tensor, first_c, square_c, gains, scales, shifts, cell_count)
    d_act = convolve(pad_both(upstream), flipped)
    d_pre = d_act * silu_slope(pre_act)

    def mapping(tensor_v, first_v, square_v, gains_v, scales_v, shifts_v):
        return normalize_spread(tensor_v, first_v, square_v, gains_v, scales_v, shifts_v, cell_count)

    _, pull_back = jax.vjp(mapping, tensor, first_c, square_c, gains, scales, shifts)
    d_tensor, d_first, d_square, d_gains, d_scales, d_shifts = pull_back(d_pre)
    d_first = over_groups(d_first, blocks)[:, None, None, :]
    d_square = over_groups(d_square, blocks)[:, None, None, :]
    d_tensor = d_tensor + d_first + 2.0 * tensor * d_square
    d_input = (upstream.astype(jnp.float32) + d_tensor).astype(jnp.bfloat16)
    return d_input, (d_gains, d_scales, d_shifts)


def keep(flag, new, old):
    return jax.tree.map(lambda a, b: jnp.where(flag, a, b), new, old)


def per_device(images, steps, out_grad, conv_weight, gn_gain, emb_weight):
    section_count = lax.axis_size("section")
    section_no = lax.axis_index("section")
    images = lax.all_gather(images, "space", axis=1, tiled=True)
    out_grad = lax.all_gather(out_grad, "space", axis=1, tiled=True)
    row_count = images.shape[1]
    col_count = images.shape[2]
    channels = images.shape[3]
    cell_count = row_count * col_count * (channels // G)
    weight = conv_weight[0]
    flat_weight = weight.reshape(9 * channels, channels)
    flipped = flip_weight(weight)
    gains = gn_gain[0]
    features = sinusoid(steps, FREQ)
    embedded = jnp.dot(features, emb_weight[0].astype(jnp.float32), precision=lax.Precision.HIGHEST)
    scales = embedded[:, :channels]
    shifts = embedded[:, channels:]
    last = section_count - 1
    carried = images
    kept = None
    for moment in range(section_count):
        inputs = images
        if moment > 0:
            inputs = lax.ppermute(carried, "section", [(moment - 1, moment)])
        if moment == last:
            inputs = (inputs.astype(jnp.float32) + skip.astype(jnp.float32)).astype(jnp.bfloat16)
        output, saved = block_forward(inputs, flat_weight, gains, scales, shifts, cell_count)
        if moment == 0:
            skip = lax.ppermute(output, "section", [(0, last)])
        state = (inputs, saved)
        kept = state if kept is None else keep(section_no == moment, state, kept)
        carried = output
    kept_in, kept_saved = kept
    carried = out_grad
    kept = None
    for moment in range(section_count):
        active = last - moment
        upstream = out_grad
        if moment > 0:
            upstream = lax.ppermute(carried, "section", [(active + 1, active)])
        if active == 0:
            upstream = (upstream.astype(jnp.float32) + skip_grad.astype(jnp.float32)).astype(
                jnp.bfloat16
            )
        d_input, pieces = block_backward(
            upstream, kept_in, kept_saved, flipped, gains, scales, shifts, cell_count
        )
        if moment == 0:
            skip_grad = lax.ppermute(d_input, "section", [(last, 0)])
        state = (upstream, pieces)
        kept = state if kept is None else keep(section_no == active, state, kept)
        carried = d_input
    kept_up, (d_gains, d_scales, d_shifts) = kept
    space_count = lax.axis_size("space")
    space_no = quarter_of(lax.axis_index("space"), space_count)
    patch_rows = 9 * channels // space_count
    flat_patch = patches(kept_saved[2], row_count, col_count).reshape(-1, 9 * channels)
    own_patch = lax.dynamic_slice_in_dim(flat_patch, space_no * patch_rows, patch_rows, axis=1)
    weight_grad = jnp.dot(
        own_patch.T, kept_up.reshape(-1, channels), preferred_element_type=jnp.float32
    )
    emb_rows = FREQ // space_count
    own_features = lax.dynamic_slice_in_dim(features, space_no * emb_rows, emb_rows, axis=1)
    emb_grad = jnp.dot(
        own_features.T,
        jnp.concatenate([d_scales, d_shifts], axis=1),
        precision=lax.Precision.HIGHEST,
    )
    return reduce_grads(weight_grad, d_gains, emb_grad)


def butterfly_scatter(flat, axis):
    count = lax.axis_size(axis)
    index = lax.axis_index(axis)
    step = 1
    while step < count:
        bit = (index // step) % 2
        half = flat.shape[0] // 2
        kept = lax.dynamic_slice_in_dim(flat, bit * half, half, 0)
        sent = lax.dynamic_slice_in_dim(flat, (1 - bit) * half, half, 0)
        flat = kept + lax.ppermute(sent, axis, [(j, j ^ step) for j in range(count)])
        step *= 2
    return flat


def butterfly_sum(flat, axis):
    count = lax.axis_size(axis)
    step = 1
    while step < count:
        flat = flat + lax.ppermute(flat, axis, [(j, j ^ step) for j in range(count)])
        step *= 2
    return flat


def butterfly_gather(flat, axis, steps):
    count = lax.axis_size(axis)
    index = lax.axis_index(axis)
    for step in steps:
        bit = (index // step) % 2
        got = lax.ppermute(flat, axis, [(j, j ^ step) for j in range(count)])
        flat = jnp.where(bit == 1, jnp.concatenate([got, flat]), jnp.concatenate([flat, got]))
    return flat


def descending(count):
    steps = []
    step = count // 2
    while step >= 1:
        steps.append(step)
        step //= 2
    return steps


def quarter_of(space_no, space_count):
    return (space_no % 2) * (space_count // 2) + space_no // 2


def reduce_grads(weight_grad, gain_grad, emb_grad):
    channels = gain_grad.shape[0]
    parts = [weight_grad, emb_grad.reshape(-1, channels), gain_grad[None]]
    rows = sum(part.shape[0] for part in parts)
    devices = lax.axis_size("dx")
    padded_rows = -(-rows // (8 * devices)) * 8 * devices
    parts.append(jnp.zeros((padded_rows - rows, channels), jnp.float32))
    flat = jnp.concatenate(parts, axis=0)
    flat = butterfly_scatter(flat, "dx")
    flat = butterfly_sum(flat, "dy")
    flat = butterfly_gather(flat.astype(jnp.bfloat16), "dx", descending(lax.axis_size("dx")))
    space_count = lax.axis_size("space")
    flat = butterfly_gather(flat, "space", descending(space_count))
    flat = flat.reshape(space_count, padded_rows, channels).astype(jnp.float32)
    weight_rows = weight_grad.shape[0]
    emb_rows = emb_grad.size // channels
    conv = flat[:, :weight_rows].reshape(1, 3, 3, channels, channels)
    emb = flat[:, weight_rows : weight_rows + emb_rows].reshape(1, emb_grad.shape[0] * space_count, -1)
    gain = flat[0, weight_rows + emb_rows][None]
    return (conv, gain, emb)


def solution(mesh):
    dp_n = mesh.shape["dp"]
    dx_n = 4 if dp_n % 4 == 0 else 1
    mesh = Mesh(
        mesh.devices.reshape(dp_n // dx_n, dx_n, *mesh.devices.shape[1:]),
        ("dy", "dx", "section", "space"),
    )
    data = ("dy", "dx")
    in_specs = (
        P(data, "space", None, None),
        P(data),
        P(data, "space", None, None),
        P("section", None, None, None, None),
        P("section", None),
        P("section", None, None),
    )
    out_specs = (P("section", None, None, None, None), P("section", None), P("section", None, None))
    return jax.shard_map(
        per_device, mesh=mesh, in_specs=in_specs, out_specs=out_specs, check_vma=False
    )
```

```python
import math

import jax
import jax.numpy as jnp
from jax import lax
from jax.sharding import Mesh, PartitionSpec as P

G = 32
FREQ = 256
MICRO = 2


EPS = 1e-05


def from_behind(value, axis, steps):
    count = lax.axis_size(axis)
    initial, last = (max(0, -steps), min(count, count - steps))
    return lax.ppermute(value, axis, [(source, source + steps) for source in range(initial, last)])


def extended(shard, sides, width):
    for axis, dim in sides:
        size, length = (lax.axis_size(axis), shard.shape[dim])
        up = [(i, (i + 1) % size) for i in range(size - 1)]
        down = [(j, i) for i, j in up]
        last = lax.slice_in_dim(shard, length - width, length, axis=dim)
        initial = lax.slice_in_dim(shard, 0, width, axis=dim)
        before = lax.ppermute(last, axis, up)
        after = lax.ppermute(initial, axis, down)
        shard = jnp.concatenate([before, shard, after], axis=dim)
    return shard


def sinusoid(timesteps, feature_n):
    half_n = feature_n // 2
    freqs = jnp.exp(-math.log(10000.0) * jnp.arange(half_n, dtype=jnp.float32) / half_n)
    angles = timesteps.astype(jnp.float32)[:, None] * freqs[None, :]
    return jnp.concatenate([jnp.cos(angles), jnp.sin(angles)], axis=1)


def group_sums(tensor, groups):
    batch_n, height_n, width_n, channels = tensor.shape
    split = tensor.reshape(batch_n, height_n, width_n, groups, channels // groups)
    return (jnp.sum(split, axis=(1, 2, 4)), jnp.sum(split * split, axis=(1, 2, 4)))


def spread(values, channels):
    return jnp.repeat(values, channels // values.shape[1], axis=1)[:, None, None, :]


def normalize(tensor, first_sum, square_sum, gains, scales, shifts, cell_count):
    channels = tensor.shape[3]
    average = first_sum / cell_count
    inverse = lax.rsqrt(square_sum / cell_count - average * average + EPS)
    normed = (tensor - spread(average, channels)) * spread(inverse, channels) * gains
    return normed * (1.0 + scales[:, None, None, :]) + shifts[:, None, None, :]


def patches(padded, height_n, width_n):
    return jnp.concatenate(
        [
            padded[:, vertical : vertical + height_n, lateral : lateral + width_n, :]
            for vertical in range(3)
            for lateral in range(3)
        ],
        axis=3,
    )


def convolve(padded, matrix):
    batch_n, height_p, width_p, channels = padded.shape
    flat = patches(padded, height_p - 2, width_p - 2).reshape(-1, 9 * channels)
    return jnp.dot(flat, matrix, preferred_element_type=jnp.float32).reshape(
        batch_n, height_p - 2, width_p - 2, matrix.shape[1]
    )


def flip_weight(weight):
    channels = weight.shape[2]
    return jnp.transpose(weight[::-1, ::-1], (0, 1, 3, 2)).reshape(9 * channels, channels)


def silu_slope(pre_act):
    sigmoid_v = jax.nn.sigmoid(pre_act)
    return sigmoid_v * (1.0 + pre_act * (1.0 - sigmoid_v))


def pad_columns(tensor):
    return jnp.pad(tensor, ((0, 0), (0, 0), (1, 1), (0, 0)))


def pick(stacked, index):
    return lax.dynamic_index_in_dim(stacked, index, 0, keepdims=False)


def norm_backward(tensor, first_sum, square_sum, gains, scales, shifts, cell_count, d_pre):

    def mapping(tensor_v, first_v, square_v, gains_v, scales_v, shifts_v):
        return normalize(tensor_v, first_v, square_v, gains_v, scales_v, shifts_v, cell_count)

    _, pull_back = jax.vjp(mapping, tensor, first_sum, square_sum, gains, scales, shifts)
    return pull_back(d_pre)


def pad_both(tensor):
    return jnp.pad(tensor, ((0, 0), (1, 1), (1, 1), (0, 0)))


def group_blocks(channels):
    group = jnp.arange(channels) // (channels // G)
    return (group[:, None] == group[None, :]).astype(jnp.float32)


def over_groups(values, blocks):
    return jnp.dot(values, blocks, precision=lax.Precision.HIGHEST)


def normalize_spread(tensor, first_c, square_c, gains, scales, shifts, cell_count):
    average = first_c / cell_count
    inverse = lax.rsqrt(square_c / cell_count - average * average + EPS)
    normed = (tensor - average[:, None, None, :]) * inverse[:, None, None, :] * gains
    return normed * (1.0 + scales[:, None, None, :]) + shifts[:, None, None, :]


def block_forward(inputs, flat_weight, gains, scales, shifts, cell_count):
    tensor = inputs.astype(jnp.float32)
    blocks = group_blocks(tensor.shape[3])
    first_c = over_groups(jnp.sum(tensor, axis=(1, 2)), blocks)
    square_c = over_groups(jnp.sum(tensor * tensor, axis=(1, 2)), blocks)
    pre_act = normalize_spread(tensor, first_c, square_c, gains, scales, shifts, cell_count)
    activation = jax.nn.silu(pre_act).astype(jnp.bfloat16)
    padded = pad_both(activation)
    output = (tensor + convolve(padded, flat_weight)).astype(jnp.bfloat16)
    return output, (first_c, square_c, padded)


def block_backward(upstream, inputs, saved, flipped, gains, scales, shifts, cell_count):
    first_c, square_c, _ = saved
    tensor = inputs.astype(jnp.float32)
    blocks = group_blocks(tensor.shape[3])
    pre_act = normalize_spread(tensor, first_c, square_c, gains, scales, shifts, cell_count)
    d_act = convolve(pad_both(upstream), flipped)
    d_pre = d_act * silu_slope(pre_act)

    def mapping(tensor_v, first_v, square_v, gains_v, scales_v, shifts_v):
        return normalize_spread(tensor_v, first_v, square_v, gains_v, scales_v, shifts_v, cell_count)

    _, pull_back = jax.vjp(mapping, tensor, first_c, square_c, gains, scales, shifts)
    d_tensor, d_first, d_square, d_gains, d_scales, d_shifts = pull_back(d_pre)
    d_first = over_groups(d_first, blocks)[:, None, None, :]
    d_square = over_groups(d_square, blocks)[:, None, None, :]
    d_tensor = d_tensor + d_first + 2.0 * tensor * d_square
    d_input = (upstream.astype(jnp.float32) + d_tensor).astype(jnp.bfloat16)
    return d_input, (d_gains, d_scales, d_shifts)


def keep(flag, new, old):
    return jax.tree.map(lambda a, b: jnp.where(flag, a, b), new, old)


def per_device(images, steps, out_grad, conv_weight, gn_gain, emb_weight):
    section_count = lax.axis_size("section")
    section_no = lax.axis_index("section")
    both = lax.all_gather(jnp.stack([images, out_grad]), "space", axis=2, tiled=True)
    images = both[0]
    out_grad = both[1]
    row_count = images.shape[1]
    col_count = images.shape[2]
    channels = images.shape[3]
    cell_count = row_count * col_count * (channels // G)
    weight = conv_weight[0]
    flat_weight = weight.reshape(9 * channels, channels)
    flipped = flip_weight(weight)
    gains = gn_gain[0]
    features = sinusoid(steps, FREQ)
    embedded = jnp.dot(features, emb_weight[0].astype(jnp.float32), precision=lax.Precision.HIGHEST)
    scales = embedded[:, :channels]
    shifts = embedded[:, channels:]
    last = section_count - 1
    carried = images
    kept = None
    for moment in range(section_count):
        inputs = images
        if moment > 0:
            inputs = lax.ppermute(carried, "section", [(moment - 1, moment)])
        if moment == last:
            inputs = (inputs.astype(jnp.float32) + skip.astype(jnp.float32)).astype(jnp.bfloat16)
        output, saved = block_forward(inputs, flat_weight, gains, scales, shifts, cell_count)
        if moment == 0:
            skip = lax.ppermute(output, "section", [(0, last)])
        state = (inputs, saved)
        kept = state if kept is None else keep(section_no == moment, state, kept)
        carried = output
    kept_in, kept_saved = kept
    carried = out_grad
    kept = None
    for moment in range(section_count):
        active = last - moment
        upstream = out_grad
        if moment > 0:
            upstream = lax.ppermute(carried, "section", [(active + 1, active)])
        if active == 0:
            upstream = (upstream.astype(jnp.float32) + skip_grad.astype(jnp.float32)).astype(
                jnp.bfloat16
            )
        d_input, pieces = block_backward(
            upstream, kept_in, kept_saved, flipped, gains, scales, shifts, cell_count
        )
        if moment == 0:
            skip_grad = lax.ppermute(d_input, "section", [(last, 0)])
        state = (upstream, pieces)
        kept = state if kept is None else keep(section_no == active, state, kept)
        carried = d_input
    kept_up, (d_gains, d_scales, d_shifts) = kept
    space_count = lax.axis_size("space")
    space_no = quarter_of(lax.axis_index("space"), space_count)
    patch_rows = 9 * channels // space_count
    flat_patch = patches(kept_saved[2], row_count, col_count).reshape(-1, 9 * channels)
    own_patch = lax.dynamic_slice_in_dim(flat_patch, space_no * patch_rows, patch_rows, axis=1)
    weight_grad = jnp.dot(
        own_patch.T, kept_up.reshape(-1, channels), preferred_element_type=jnp.float32
    )
    emb_rows = FREQ // space_count
    own_features = lax.dynamic_slice_in_dim(features, space_no * emb_rows, emb_rows, axis=1)
    emb_grad = jnp.dot(
        own_features.T,
        jnp.concatenate([d_scales, d_shifts], axis=1),
        precision=lax.Precision.HIGHEST,
    )
    return reduce_grads(weight_grad, d_gains, emb_grad)


def butterfly_scatter(flat, axis):
    count = lax.axis_size(axis)
    index = lax.axis_index(axis)
    step = 1
    while step < count:
        bit = (index // step) % 2
        half = flat.shape[0] // 2
        kept = lax.dynamic_slice_in_dim(flat, bit * half, half, 0)
        sent = lax.dynamic_slice_in_dim(flat, (1 - bit) * half, half, 0)
        flat = kept + lax.ppermute(sent, axis, [(j, j ^ step) for j in range(count)])
        step *= 2
    return flat


def butterfly_sum(flat, axis):
    count = lax.axis_size(axis)
    step = 1
    while step < count:
        flat = flat + lax.ppermute(flat, axis, [(j, j ^ step) for j in range(count)])
        step *= 2
    return flat


def butterfly_gather(flat, axis, steps):
    count = lax.axis_size(axis)
    index = lax.axis_index(axis)
    for step in steps:
        bit = (index // step) % 2
        got = lax.ppermute(flat, axis, [(j, j ^ step) for j in range(count)])
        flat = jnp.where(bit == 1, jnp.concatenate([got, flat]), jnp.concatenate([flat, got]))
    return flat


def descending(count):
    steps = []
    step = count // 2
    while step >= 1:
        steps.append(step)
        step //= 2
    return steps


def quarter_of(space_no, space_count):
    return (space_no % 2) * (space_count // 2) + space_no // 2


def reduce_grads(weight_grad, gain_grad, emb_grad):
    channels = gain_grad.shape[0]
    parts = [weight_grad, emb_grad.reshape(-1, channels), gain_grad[None]]
    rows = sum(part.shape[0] for part in parts)
    devices = lax.axis_size("dx")
    padded_rows = -(-rows // (8 * devices)) * 8 * devices
    parts.append(jnp.zeros((padded_rows - rows, channels), jnp.float32))
    flat = jnp.concatenate(parts, axis=0)
    flat = butterfly_scatter(flat, "dx")
    flat = butterfly_sum(flat, "dy")
    flat = butterfly_gather(flat.astype(jnp.bfloat16), "dx", descending(lax.axis_size("dx")))
    space_count = lax.axis_size("space")
    flat = butterfly_gather(flat, "space", descending(space_count))
    flat = flat.reshape(space_count, padded_rows, channels).astype(jnp.float32)
    weight_rows = weight_grad.shape[0]
    emb_rows = emb_grad.size // channels
    conv = flat[:, :weight_rows].reshape(1, 3, 3, channels, channels)
    emb = flat[:, weight_rows : weight_rows + emb_rows].reshape(1, emb_grad.shape[0] * space_count, -1)
    gain = flat[0, weight_rows + emb_rows][None]
    return (conv, gain, emb)


def solution(mesh):
    dp_n = mesh.shape["dp"]
    dx_n = 4 if dp_n % 4 == 0 else 1
    mesh = Mesh(
        mesh.devices.reshape(dp_n // dx_n, dx_n, *mesh.devices.shape[1:]),
        ("dy", "dx", "section", "space"),
    )
    data = ("dy", "dx")
    in_specs = (
        P(data, "space", None, None),
        P(data),
        P(data, "space", None, None),
        P("section", None, None, None, None),
        P("section", None),
        P("section", None, None),
    )
    out_specs = (P("section", None, None, None, None), P("section", None), P("section", None, None))
    return jax.shard_map(
        per_device, mesh=mesh, in_specs=in_specs, out_specs=out_specs, check_vma=False
    )
```

```python
import math

import jax
import jax.numpy as jnp
from jax import lax
from jax.sharding import Mesh, PartitionSpec as P

G = 32
FREQ = 256
MICRO = 2


EPS = 1e-05


def from_behind(value, axis, steps):
    count = lax.axis_size(axis)
    initial, last = (max(0, -steps), min(count, count - steps))
    return lax.ppermute(value, axis, [(source, source + steps) for source in range(initial, last)])


def extended(shard, sides, width):
    for axis, dim in sides:
        size, length = (lax.axis_size(axis), shard.shape[dim])
        up = [(i, (i + 1) % size) for i in range(size - 1)]
        down = [(j, i) for i, j in up]
        last = lax.slice_in_dim(shard, length - width, length, axis=dim)
        initial = lax.slice_in_dim(shard, 0, width, axis=dim)
        before = lax.ppermute(last, axis, up)
        after = lax.ppermute(initial, axis, down)
        shard = jnp.concatenate([before, shard, after], axis=dim)
    return shard


def sinusoid(timesteps, feature_n):
    half_n = feature_n // 2
    freqs = jnp.exp(-math.log(10000.0) * jnp.arange(half_n, dtype=jnp.float32) / half_n)
    angles = timesteps.astype(jnp.float32)[:, None] * freqs[None, :]
    return jnp.concatenate([jnp.cos(angles), jnp.sin(angles)], axis=1)


def group_sums(tensor, groups):
    batch_n, height_n, width_n, channels = tensor.shape
    split = tensor.reshape(batch_n, height_n, width_n, groups, channels // groups)
    return (jnp.sum(split, axis=(1, 2, 4)), jnp.sum(split * split, axis=(1, 2, 4)))


def spread(values, channels):
    return jnp.repeat(values, channels // values.shape[1], axis=1)[:, None, None, :]


def normalize(tensor, first_sum, square_sum, gains, scales, shifts, cell_count):
    channels = tensor.shape[3]
    average = first_sum / cell_count
    inverse = lax.rsqrt(square_sum / cell_count - average * average + EPS)
    normed = (tensor - spread(average, channels)) * spread(inverse, channels) * gains
    return normed * (1.0 + scales[:, None, None, :]) + shifts[:, None, None, :]


def patches(padded, height_n, width_n):
    return jnp.concatenate(
        [
            padded[:, vertical : vertical + height_n, lateral : lateral + width_n, :]
            for vertical in range(3)
            for lateral in range(3)
        ],
        axis=3,
    )


def convolve(padded, matrix):
    batch_n, height_p, width_p, channels = padded.shape
    flat = patches(padded, height_p - 2, width_p - 2).reshape(-1, 9 * channels)
    return jnp.dot(flat, matrix, preferred_element_type=jnp.float32).reshape(
        batch_n, height_p - 2, width_p - 2, matrix.shape[1]
    )


def flip_weight(weight):
    channels = weight.shape[2]
    return jnp.transpose(weight[::-1, ::-1], (0, 1, 3, 2)).reshape(9 * channels, channels)


def silu_slope(pre_act):
    sigmoid_v = jax.nn.sigmoid(pre_act)
    return sigmoid_v * (1.0 + pre_act * (1.0 - sigmoid_v))


def pad_columns(tensor):
    return jnp.pad(tensor, ((0, 0), (0, 0), (1, 1), (0, 0)))


def pick(stacked, index):
    return lax.dynamic_index_in_dim(stacked, index, 0, keepdims=False)


def norm_backward(tensor, first_sum, square_sum, gains, scales, shifts, cell_count, d_pre):

    def mapping(tensor_v, first_v, square_v, gains_v, scales_v, shifts_v):
        return normalize(tensor_v, first_v, square_v, gains_v, scales_v, shifts_v, cell_count)

    _, pull_back = jax.vjp(mapping, tensor, first_sum, square_sum, gains, scales, shifts)
    return pull_back(d_pre)


def pad_both(tensor):
    return jnp.pad(tensor, ((0, 0), (1, 1), (1, 1), (0, 0)))


def group_blocks(channels):
    group = jnp.arange(channels) // (channels // G)
    return (group[:, None] == group[None, :]).astype(jnp.float32)


def over_groups(values, blocks):
    return jnp.dot(values, blocks, precision=lax.Precision.HIGHEST)


def normalize_spread(tensor, first_c, square_c, gains, scales, shifts, cell_count):
    average = first_c / cell_count
    inverse = lax.rsqrt(square_c / cell_count - average * average + EPS)
    normed = (tensor - average[:, None, None, :]) * inverse[:, None, None, :] * gains
    return normed * (1.0 + scales[:, None, None, :]) + shifts[:, None, None, :]


def block_forward(inputs, flat_weight, gains, scales, shifts, cell_count):
    tensor = inputs.astype(jnp.float32)
    blocks = group_blocks(tensor.shape[3])
    first_c = over_groups(jnp.sum(tensor, axis=(1, 2)), blocks)
    square_c = over_groups(jnp.sum(tensor * tensor, axis=(1, 2)), blocks)
    pre_act = normalize_spread(tensor, first_c, square_c, gains, scales, shifts, cell_count)
    activation = jax.nn.silu(pre_act).astype(jnp.bfloat16)
    padded = pad_both(activation)
    output = (tensor + convolve(padded, flat_weight)).astype(jnp.bfloat16)
    return output, (first_c, square_c, padded)


def block_backward(upstream, inputs, saved, flipped, gains, scales, shifts, cell_count):
    first_c, square_c, _ = saved
    tensor = inputs.astype(jnp.float32)
    blocks = group_blocks(tensor.shape[3])
    pre_act = normalize_spread(tensor, first_c, square_c, gains, scales, shifts, cell_count)
    d_act = convolve(pad_both(upstream), flipped)
    d_pre = d_act * silu_slope(pre_act)

    def mapping(tensor_v, first_v, square_v, gains_v, scales_v, shifts_v):
        return normalize_spread(tensor_v, first_v, square_v, gains_v, scales_v, shifts_v, cell_count)

    _, pull_back = jax.vjp(mapping, tensor, first_c, square_c, gains, scales, shifts)
    d_tensor, d_first, d_square, d_gains, d_scales, d_shifts = pull_back(d_pre)
    d_first = over_groups(d_first, blocks)[:, None, None, :]
    d_square = over_groups(d_square, blocks)[:, None, None, :]
    d_tensor = d_tensor + d_first + 2.0 * tensor * d_square
    d_input = (upstream.astype(jnp.float32) + d_tensor).astype(jnp.bfloat16)
    return d_input, (d_gains, d_scales, d_shifts)


def keep(flag, new, old):
    return jax.tree.map(lambda a, b: jnp.where(flag, a, b), new, old)


def per_device(images, steps, out_grad, conv_weight, gn_gain, emb_weight):
    section_count = lax.axis_size("section")
    section_no = lax.axis_index("section")
    images = lax.all_gather(images, "space", axis=1, tiled=True)
    out_grad = lax.all_gather(out_grad, "space", axis=1, tiled=True)
    row_count = images.shape[1]
    col_count = images.shape[2]
    channels = images.shape[3]
    cell_count = row_count * col_count * (channels // G)
    weight = conv_weight[0]
    flat_weight = weight.reshape(9 * channels, channels)
    flipped = flip_weight(weight)
    gains = gn_gain[0]
    features = sinusoid(steps, FREQ)
    embedded = jnp.dot(features, emb_weight[0].astype(jnp.float32), precision=lax.Precision.HIGHEST)
    scales = embedded[:, :channels]
    shifts = embedded[:, channels:]
    last = section_count - 1
    carried = images
    kept = None
    for moment in range(section_count):
        inputs = images
        if moment > 0:
            inputs = lax.ppermute(carried, "section", [(moment - 1, moment)])
        if moment == last:
            inputs = (inputs.astype(jnp.float32) + skip.astype(jnp.float32)).astype(jnp.bfloat16)
        output, saved = block_forward(inputs, flat_weight, gains, scales, shifts, cell_count)
        if moment == 0:
            skip = lax.ppermute(output, "section", [(0, last)])
        state = (inputs, saved)
        kept = state if kept is None else keep(section_no == moment, state, kept)
        carried = output
    kept_in, kept_saved = kept
    carried = out_grad
    kept = None
    for moment in range(section_count):
        active = last - moment
        upstream = out_grad
        if moment > 0:
            upstream = lax.ppermute(carried, "section", [(active + 1, active)])
        if active == 0:
            upstream = (upstream.astype(jnp.float32) + skip_grad.astype(jnp.float32)).astype(
                jnp.bfloat16
            )
        d_input, pieces = block_backward(
            upstream, kept_in, kept_saved, flipped, gains, scales, shifts, cell_count
        )
        if moment == 0:
            skip_grad = lax.ppermute(d_input, "section", [(last, 0)])
        state = (upstream, pieces)
        kept = state if kept is None else keep(section_no == active, state, kept)
        carried = d_input
    kept_up, (d_gains, d_scales, d_shifts) = kept
    space_count = lax.axis_size("space")
    space_no = quarter_of(lax.axis_index("space"), space_count)
    patch_rows = 9 * channels // space_count
    flat_patch = patches(kept_saved[2], row_count, col_count).reshape(-1, 9 * channels)
    own_patch = lax.dynamic_slice_in_dim(flat_patch, space_no * patch_rows, patch_rows, axis=1)
    weight_grad = jnp.dot(
        own_patch.T, kept_up.reshape(-1, channels), preferred_element_type=jnp.float32
    )
    emb_rows = FREQ // space_count
    own_features = lax.dynamic_slice_in_dim(features, space_no * emb_rows, emb_rows, axis=1)
    emb_grad = jnp.dot(
        own_features.T,
        jnp.concatenate([d_scales, d_shifts], axis=1),
        precision=lax.Precision.HIGHEST,
    )
    return reduce_grads(weight_grad, d_gains, emb_grad)


def butterfly_scatter(flat, axis):
    count = lax.axis_size(axis)
    index = lax.axis_index(axis)
    step = 1
    while step < count:
        bit = (index // step) % 2
        half = flat.shape[0] // 2
        kept = lax.dynamic_slice_in_dim(flat, bit * half, half, 0)
        sent = lax.dynamic_slice_in_dim(flat, (1 - bit) * half, half, 0)
        flat = kept + lax.ppermute(sent, axis, [(j, j ^ step) for j in range(count)])
        step *= 2
    return flat


def butterfly_sum(flat, axis):
    count = lax.axis_size(axis)
    step = 1
    while step < count:
        flat = flat + lax.ppermute(flat, axis, [(j, j ^ step) for j in range(count)])
        step *= 2
    return flat


def butterfly_gather(flat, axis, steps, dim=0):
    count = lax.axis_size(axis)
    index = lax.axis_index(axis)
    for step in steps:
        bit = (index // step) % 2
        got = lax.ppermute(flat, axis, [(j, j ^ step) for j in range(count)])
        flat = jnp.where(
            bit == 1, jnp.concatenate([got, flat], axis=dim), jnp.concatenate([flat, got], axis=dim)
        )
    return flat


def descending(count):
    steps = []
    step = count // 2
    while step >= 1:
        steps.append(step)
        step //= 2
    return steps


def quarter_of(space_no, space_count):
    return (space_no % 2) * (space_count // 2) + space_no // 2


def reduce_grads(weight_grad, gain_grad, emb_grad):
    channels = gain_grad.shape[0]
    parts = [weight_grad, emb_grad.reshape(-1, channels), gain_grad[None]]
    rows = sum(part.shape[0] for part in parts)
    devices = lax.axis_size("dx")
    padded_rows = -(-rows // (8 * devices)) * 8 * devices
    parts.append(jnp.zeros((padded_rows - rows, channels), jnp.float32))
    flat = jnp.concatenate(parts, axis=0)
    flat = butterfly_scatter(flat, "dx")
    flat = butterfly_sum(flat, "dy")
    space_count = lax.axis_size("space")
    flat = butterfly_gather(flat.astype(jnp.bfloat16), "space", descending(space_count))
    flat = flat.reshape(space_count, -1, channels)
    flat = butterfly_gather(flat, "dx", descending(lax.axis_size("dx")), dim=1)
    flat = flat.astype(jnp.float32)
    weight_rows = weight_grad.shape[0]
    emb_rows = emb_grad.size // channels
    conv = flat[:, :weight_rows].reshape(1, 3, 3, channels, channels)
    emb = flat[:, weight_rows : weight_rows + emb_rows].reshape(1, emb_grad.shape[0] * space_count, -1)
    gain = flat[0, weight_rows + emb_rows][None]
    return (conv, gain, emb)


def solution(mesh):
    dp_n = mesh.shape["dp"]
    dx_n = 4 if dp_n % 4 == 0 else 1
    mesh = Mesh(
        mesh.devices.reshape(dp_n // dx_n, dx_n, *mesh.devices.shape[1:]),
        ("dy", "dx", "section", "space"),
    )
    data = ("dy", "dx")
    in_specs = (
        P(data, "space", None, None),
        P(data),
        P(data, "space", None, None),
        P("section", None, None, None, None),
        P("section", None),
        P("section", None, None),
    )
    out_specs = (P("section", None, None, None, None), P("section", None), P("section", None, None))
    return jax.shard_map(
        per_device, mesh=mesh, in_specs=in_specs, out_specs=out_specs, check_vma=False
    )
```

```python
import math

import jax
import jax.numpy as jnp
from jax import lax
from jax.sharding import Mesh, PartitionSpec as P

G = 32
FREQ = 256
MICRO = 2


EPS = 1e-05


def from_behind(value, axis, steps):
    count = lax.axis_size(axis)
    initial, last = (max(0, -steps), min(count, count - steps))
    return lax.ppermute(value, axis, [(source, source + steps) for source in range(initial, last)])


def extended(shard, sides, width):
    for axis, dim in sides:
        size, length = (lax.axis_size(axis), shard.shape[dim])
        up = [(i, (i + 1) % size) for i in range(size - 1)]
        down = [(j, i) for i, j in up]
        last = lax.slice_in_dim(shard, length - width, length, axis=dim)
        initial = lax.slice_in_dim(shard, 0, width, axis=dim)
        before = lax.ppermute(last, axis, up)
        after = lax.ppermute(initial, axis, down)
        shard = jnp.concatenate([before, shard, after], axis=dim)
    return shard


def sinusoid(timesteps, feature_n):
    half_n = feature_n // 2
    freqs = jnp.exp(-math.log(10000.0) * jnp.arange(half_n, dtype=jnp.float32) / half_n)
    angles = timesteps.astype(jnp.float32)[:, None] * freqs[None, :]
    return jnp.concatenate([jnp.cos(angles), jnp.sin(angles)], axis=1)


def group_sums(tensor, groups):
    batch_n, height_n, width_n, channels = tensor.shape
    split = tensor.reshape(batch_n, height_n, width_n, groups, channels // groups)
    return (jnp.sum(split, axis=(1, 2, 4)), jnp.sum(split * split, axis=(1, 2, 4)))


def spread(values, channels):
    return jnp.repeat(values, channels // values.shape[1], axis=1)[:, None, None, :]


def normalize(tensor, first_sum, square_sum, gains, scales, shifts, cell_count):
    channels = tensor.shape[3]
    average = first_sum / cell_count
    inverse = lax.rsqrt(square_sum / cell_count - average * average + EPS)
    normed = (tensor - spread(average, channels)) * spread(inverse, channels) * gains
    return normed * (1.0 + scales[:, None, None, :]) + shifts[:, None, None, :]


def patches(padded, height_n, width_n):
    return jnp.concatenate(
        [
            padded[:, vertical : vertical + height_n, lateral : lateral + width_n, :]
            for vertical in range(3)
            for lateral in range(3)
        ],
        axis=3,
    )


def convolve(padded, matrix):
    batch_n, height_p, width_p, channels = padded.shape
    flat = patches(padded, height_p - 2, width_p - 2).reshape(-1, 9 * channels)
    return jnp.dot(flat, matrix, preferred_element_type=jnp.float32).reshape(
        batch_n, height_p - 2, width_p - 2, matrix.shape[1]
    )


def flip_weight(weight):
    channels = weight.shape[2]
    return jnp.transpose(weight[::-1, ::-1], (0, 1, 3, 2)).reshape(9 * channels, channels)


def silu_slope(pre_act):
    sigmoid_v = jax.nn.sigmoid(pre_act)
    return sigmoid_v * (1.0 + pre_act * (1.0 - sigmoid_v))


def pad_columns(tensor):
    return jnp.pad(tensor, ((0, 0), (0, 0), (1, 1), (0, 0)))


def pick(stacked, index):
    return lax.dynamic_index_in_dim(stacked, index, 0, keepdims=False)


def norm_backward(tensor, first_sum, square_sum, gains, scales, shifts, cell_count, d_pre):

    def mapping(tensor_v, first_v, square_v, gains_v, scales_v, shifts_v):
        return normalize(tensor_v, first_v, square_v, gains_v, scales_v, shifts_v, cell_count)

    _, pull_back = jax.vjp(mapping, tensor, first_sum, square_sum, gains, scales, shifts)
    return pull_back(d_pre)


def pad_both(tensor):
    return jnp.pad(tensor, ((0, 0), (1, 1), (1, 1), (0, 0)))


def group_blocks(channels):
    group = jnp.arange(channels) // (channels // G)
    return (group[:, None] == group[None, :]).astype(jnp.float32)


def over_groups(values, blocks):
    return jnp.dot(values, blocks, precision=lax.Precision.HIGHEST)


def normalize_spread(tensor, first_c, square_c, gains, scales, shifts, cell_count):
    average = first_c / cell_count
    inverse = lax.rsqrt(square_c / cell_count - average * average + EPS)
    normed = (tensor - average[:, None, None, :]) * inverse[:, None, None, :] * gains
    return normed * (1.0 + scales[:, None, None, :]) + shifts[:, None, None, :]


def conv_same(tensor, kernel):
    return lax.conv_general_dilated(
        tensor,
        kernel,
        (1, 1),
        ((1, 1), (1, 1)),
        dimension_numbers=("NHWC", "HWIO", "NHWC"),
        preferred_element_type=jnp.float32,
    )


def block_forward(inputs, flat_weight, gains, scales, shifts, cell_count):
    tensor = inputs.astype(jnp.float32)
    blocks = group_blocks(tensor.shape[3])
    first_c = over_groups(jnp.sum(tensor, axis=(1, 2)), blocks)
    square_c = over_groups(jnp.sum(tensor * tensor, axis=(1, 2)), blocks)
    pre_act = normalize_spread(tensor, first_c, square_c, gains, scales, shifts, cell_count)
    activation = jax.nn.silu(pre_act).astype(jnp.bfloat16)
    padded = pad_both(activation)
    output = (tensor + conv_same(activation, flat_weight)).astype(jnp.bfloat16)
    return output, (first_c, square_c, padded)


def block_backward(upstream, inputs, saved, flipped, gains, scales, shifts, cell_count):
    first_c, square_c, _ = saved
    tensor = inputs.astype(jnp.float32)
    blocks = group_blocks(tensor.shape[3])
    pre_act = normalize_spread(tensor, first_c, square_c, gains, scales, shifts, cell_count)
    d_act = conv_same(upstream, flipped)
    d_pre = d_act * silu_slope(pre_act)

    def mapping(tensor_v, first_v, square_v, gains_v, scales_v, shifts_v):
        return normalize_spread(tensor_v, first_v, square_v, gains_v, scales_v, shifts_v, cell_count)

    _, pull_back = jax.vjp(mapping, tensor, first_c, square_c, gains, scales, shifts)
    d_tensor, d_first, d_square, d_gains, d_scales, d_shifts = pull_back(d_pre)
    d_first = over_groups(d_first, blocks)[:, None, None, :]
    d_square = over_groups(d_square, blocks)[:, None, None, :]
    d_tensor = d_tensor + d_first + 2.0 * tensor * d_square
    d_input = (upstream.astype(jnp.float32) + d_tensor).astype(jnp.bfloat16)
    return d_input, (d_gains, d_scales, d_shifts)


def keep(flag, new, old):
    return jax.tree.map(lambda a, b: jnp.where(flag, a, b), new, old)


def per_device(images, steps, out_grad, conv_weight, gn_gain, emb_weight):
    section_count = lax.axis_size("section")
    section_no = lax.axis_index("section")
    images = lax.all_gather(images, "space", axis=1, tiled=True)
    out_grad = lax.all_gather(out_grad, "space", axis=1, tiled=True)
    row_count = images.shape[1]
    col_count = images.shape[2]
    channels = images.shape[3]
    cell_count = row_count * col_count * (channels // G)
    weight = conv_weight[0]
    flat_weight = weight
    flipped = jnp.transpose(weight[::-1, ::-1], (0, 1, 3, 2))
    gains = gn_gain[0]
    features = sinusoid(steps, FREQ)
    embedded = jnp.dot(features, emb_weight[0].astype(jnp.float32), precision=lax.Precision.HIGHEST)
    scales = embedded[:, :channels]
    shifts = embedded[:, channels:]
    last = section_count - 1
    carried = images
    kept = None
    for moment in range(section_count):
        inputs = images
        if moment > 0:
            inputs = lax.ppermute(carried, "section", [(moment - 1, moment)])
        if moment == last:
            inputs = (inputs.astype(jnp.float32) + skip.astype(jnp.float32)).astype(jnp.bfloat16)
        output, saved = block_forward(inputs, flat_weight, gains, scales, shifts, cell_count)
        if moment == 0:
            skip = lax.ppermute(output, "section", [(0, last)])
        state = (inputs, saved)
        kept = state if kept is None else keep(section_no == moment, state, kept)
        carried = output
    kept_in, kept_saved = kept
    carried = out_grad
    kept = None
    for moment in range(section_count):
        active = last - moment
        upstream = out_grad
        if moment > 0:
            upstream = lax.ppermute(carried, "section", [(active + 1, active)])
        if active == 0:
            upstream = (upstream.astype(jnp.float32) + skip_grad.astype(jnp.float32)).astype(
                jnp.bfloat16
            )
        d_input, pieces = block_backward(
            upstream, kept_in, kept_saved, flipped, gains, scales, shifts, cell_count
        )
        if moment == 0:
            skip_grad = lax.ppermute(d_input, "section", [(last, 0)])
        state = (upstream, pieces)
        kept = state if kept is None else keep(section_no == active, state, kept)
        carried = d_input
    kept_up, (d_gains, d_scales, d_shifts) = kept
    space_count = lax.axis_size("space")
    space_no = quarter_of(lax.axis_index("space"), space_count)
    patch_rows = 9 * channels // space_count
    flat_patch = patches(kept_saved[2], row_count, col_count).reshape(-1, 9 * channels)
    own_patch = lax.dynamic_slice_in_dim(flat_patch, space_no * patch_rows, patch_rows, axis=1)
    weight_grad = jnp.dot(
        own_patch.T, kept_up.reshape(-1, channels), preferred_element_type=jnp.float32
    )
    emb_rows = FREQ // space_count
    own_features = lax.dynamic_slice_in_dim(features, space_no * emb_rows, emb_rows, axis=1)
    emb_grad = jnp.dot(
        own_features.T,
        jnp.concatenate([d_scales, d_shifts], axis=1),
        precision=lax.Precision.HIGHEST,
    )
    return reduce_grads(weight_grad, d_gains, emb_grad)


def butterfly_scatter(flat, axis):
    count = lax.axis_size(axis)
    index = lax.axis_index(axis)
    step = 1
    while step < count:
        bit = (index // step) % 2
        half = flat.shape[0] // 2
        kept = lax.dynamic_slice_in_dim(flat, bit * half, half, 0)
        sent = lax.dynamic_slice_in_dim(flat, (1 - bit) * half, half, 0)
        flat = kept + lax.ppermute(sent, axis, [(j, j ^ step) for j in range(count)])
        step *= 2
    return flat


def butterfly_sum(flat, axis):
    count = lax.axis_size(axis)
    step = 1
    while step < count:
        flat = flat + lax.ppermute(flat, axis, [(j, j ^ step) for j in range(count)])
        step *= 2
    return flat


def butterfly_gather(flat, axis, steps):
    count = lax.axis_size(axis)
    index = lax.axis_index(axis)
    for step in steps:
        bit = (index // step) % 2
        got = lax.ppermute(flat, axis, [(j, j ^ step) for j in range(count)])
        flat = jnp.where(bit == 1, jnp.concatenate([got, flat]), jnp.concatenate([flat, got]))
    return flat


def descending(count):
    steps = []
    step = count // 2
    while step >= 1:
        steps.append(step)
        step //= 2
    return steps


def quarter_of(space_no, space_count):
    return (space_no % 2) * (space_count // 2) + space_no // 2


def reduce_grads(weight_grad, gain_grad, emb_grad):
    channels = gain_grad.shape[0]
    parts = [weight_grad, emb_grad.reshape(-1, channels), gain_grad[None]]
    rows = sum(part.shape[0] for part in parts)
    devices = lax.axis_size("dx")
    padded_rows = -(-rows // (8 * devices)) * 8 * devices
    parts.append(jnp.zeros((padded_rows - rows, channels), jnp.float32))
    flat = jnp.concatenate(parts, axis=0)
    flat = butterfly_scatter(flat, "dx")
    flat = butterfly_sum(flat, "dy")
    flat = butterfly_gather(flat.astype(jnp.bfloat16), "dx", descending(lax.axis_size("dx")))
    space_count = lax.axis_size("space")
    flat = butterfly_gather(flat, "space", descending(space_count))
    flat = flat.reshape(space_count, padded_rows, channels).astype(jnp.float32)
    weight_rows = weight_grad.shape[0]
    emb_rows = emb_grad.size // channels
    conv = flat[:, :weight_rows].reshape(1, 3, 3, channels, channels)
    emb = flat[:, weight_rows : weight_rows + emb_rows].reshape(1, emb_grad.shape[0] * space_count, -1)
    gain = flat[0, weight_rows + emb_rows][None]
    return (conv, gain, emb)


def solution(mesh):
    dp_n = mesh.shape["dp"]
    dx_n = 4 if dp_n % 4 == 0 else 1
    mesh = Mesh(
        mesh.devices.reshape(dp_n // dx_n, dx_n, *mesh.devices.shape[1:]),
        ("dy", "dx", "section", "space"),
    )
    data = ("dy", "dx")
    in_specs = (
        P(data, "space", None, None),
        P(data),
        P(data, "space", None, None),
        P("section", None, None, None, None),
        P("section", None),
        P("section", None, None),
    )
    out_specs = (P("section", None, None, None, None), P("section", None), P("section", None, None))
    return jax.shard_map(
        per_device, mesh=mesh, in_specs=in_specs, out_specs=out_specs, check_vma=False
    )
```

```python
import math

import jax
import jax.numpy as jnp
from jax import lax
from jax.sharding import Mesh, PartitionSpec as P

G = 32
FREQ = 256
MICRO = 2


EPS = 1e-05


def from_behind(value, axis, steps):
    count = lax.axis_size(axis)
    initial, last = (max(0, -steps), min(count, count - steps))
    return lax.ppermute(value, axis, [(source, source + steps) for source in range(initial, last)])


def extended(shard, sides, width):
    for axis, dim in sides:
        size, length = (lax.axis_size(axis), shard.shape[dim])
        up = [(i, (i + 1) % size) for i in range(size - 1)]
        down = [(j, i) for i, j in up]
        last = lax.slice_in_dim(shard, length - width, length, axis=dim)
        initial = lax.slice_in_dim(shard, 0, width, axis=dim)
        before = lax.ppermute(last, axis, up)
        after = lax.ppermute(initial, axis, down)
        shard = jnp.concatenate([before, shard, after], axis=dim)
    return shard


def sinusoid(timesteps, feature_n):
    half_n = feature_n // 2
    freqs = jnp.exp(-math.log(10000.0) * jnp.arange(half_n, dtype=jnp.float32) / half_n)
    angles = timesteps.astype(jnp.float32)[:, None] * freqs[None, :]
    return jnp.concatenate([jnp.cos(angles), jnp.sin(angles)], axis=1)


def group_sums(tensor, groups):
    batch_n, height_n, width_n, channels = tensor.shape
    split = tensor.reshape(batch_n, height_n, width_n, groups, channels // groups)
    return (jnp.sum(split, axis=(1, 2, 4)), jnp.sum(split * split, axis=(1, 2, 4)))


def spread(values, channels):
    return jnp.repeat(values, channels // values.shape[1], axis=1)[:, None, None, :]


def normalize(tensor, first_sum, square_sum, gains, scales, shifts, cell_count):
    channels = tensor.shape[3]
    average = first_sum / cell_count
    inverse = lax.rsqrt(square_sum / cell_count - average * average + EPS)
    normed = (tensor - spread(average, channels)) * spread(inverse, channels) * gains
    return normed * (1.0 + scales[:, None, None, :]) + shifts[:, None, None, :]


def patches(padded, height_n, width_n):
    return jnp.concatenate(
        [
            padded[:, vertical : vertical + height_n, lateral : lateral + width_n, :]
            for vertical in range(3)
            for lateral in range(3)
        ],
        axis=3,
    )


def convolve(padded, matrix):
    batch_n, height_p, width_p, channels = padded.shape
    flat = patches(padded, height_p - 2, width_p - 2).reshape(-1, 9 * channels)
    return jnp.dot(flat, matrix, preferred_element_type=jnp.float32).reshape(
        batch_n, height_p - 2, width_p - 2, matrix.shape[1]
    )


def flip_weight(weight):
    channels = weight.shape[2]
    return jnp.transpose(weight[::-1, ::-1], (0, 1, 3, 2)).reshape(9 * channels, channels)


def silu_slope(pre_act):
    sigmoid_v = jax.nn.sigmoid(pre_act)
    return sigmoid_v * (1.0 + pre_act * (1.0 - sigmoid_v))


def pad_columns(tensor):
    return jnp.pad(tensor, ((0, 0), (0, 0), (1, 1), (0, 0)))


def pick(stacked, index):
    return lax.dynamic_index_in_dim(stacked, index, 0, keepdims=False)


def norm_backward(tensor, first_sum, square_sum, gains, scales, shifts, cell_count, d_pre):

    def mapping(tensor_v, first_v, square_v, gains_v, scales_v, shifts_v):
        return normalize(tensor_v, first_v, square_v, gains_v, scales_v, shifts_v, cell_count)

    _, pull_back = jax.vjp(mapping, tensor, first_sum, square_sum, gains, scales, shifts)
    return pull_back(d_pre)


def pad_both(tensor):
    return jnp.pad(tensor, ((0, 0), (1, 1), (1, 1), (0, 0)))


def group_blocks(channels):
    group = jnp.arange(channels) // (channels // G)
    return (group[:, None] == group[None, :]).astype(jnp.float32)


def over_groups(values, blocks):
    return jnp.dot(values, blocks, precision=lax.Precision.HIGHEST)


def normalize_spread(tensor, first_c, square_c, gains, scales, shifts, cell_count):
    average = first_c / cell_count
    inverse = lax.rsqrt(square_c / cell_count - average * average + EPS)
    normed = (tensor - average[:, None, None, :]) * inverse[:, None, None, :] * gains
    return normed * (1.0 + scales[:, None, None, :]) + shifts[:, None, None, :]


def conv_same(tensor, kernel):
    return lax.conv_general_dilated(
        tensor,
        kernel,
        (1, 1),
        ((1, 1), (1, 1)),
        dimension_numbers=("NHWC", "HWIO", "NHWC"),
        preferred_element_type=jnp.float32,
    )


def block_forward(inputs, flat_weight, gains, scales, shifts, cell_count):
    tensor = inputs.astype(jnp.float32)
    blocks = group_blocks(tensor.shape[3])
    first_c = over_groups(jnp.sum(tensor, axis=(1, 2)), blocks)
    square_c = over_groups(jnp.sum(tensor * tensor, axis=(1, 2)), blocks)
    pre_act = normalize_spread(tensor, first_c, square_c, gains, scales, shifts, cell_count)
    activation = jax.nn.silu(pre_act).astype(jnp.bfloat16)
    padded = pad_both(activation)
    output = (tensor + conv_same(activation, flat_weight)).astype(jnp.bfloat16)
    return output, (first_c, square_c, padded)


def block_backward(upstream, inputs, saved, flipped, gains, scales, shifts, cell_count):
    first_c, square_c, _ = saved
    tensor = inputs.astype(jnp.float32)
    blocks = group_blocks(tensor.shape[3])
    pre_act = normalize_spread(tensor, first_c, square_c, gains, scales, shifts, cell_count)
    d_act = conv_same(upstream, flipped)
    d_pre = d_act * silu_slope(pre_act)

    def mapping(tensor_v, first_v, square_v, gains_v, scales_v, shifts_v):
        return normalize_spread(tensor_v, first_v, square_v, gains_v, scales_v, shifts_v, cell_count)

    _, pull_back = jax.vjp(mapping, tensor, first_c, square_c, gains, scales, shifts)
    d_tensor, d_first, d_square, d_gains, d_scales, d_shifts = pull_back(d_pre)
    d_first = over_groups(d_first, blocks)[:, None, None, :]
    d_square = over_groups(d_square, blocks)[:, None, None, :]
    d_tensor = d_tensor + d_first + 2.0 * tensor * d_square
    d_input = (upstream.astype(jnp.float32) + d_tensor).astype(jnp.bfloat16)
    return d_input, (d_gains, d_scales, d_shifts)


def keep(flag, new, old):
    return jax.tree.map(lambda a, b: jnp.where(flag, a, b), new, old)


def per_device(images, steps, out_grad, conv_weight, gn_gain, emb_weight):
    section_count = lax.axis_size("section")
    section_no = lax.axis_index("section")
    images = lax.all_gather(images, "space", axis=1, tiled=True)
    out_grad = lax.all_gather(out_grad, "space", axis=1, tiled=True)
    row_count = images.shape[1]
    col_count = images.shape[2]
    channels = images.shape[3]
    cell_count = row_count * col_count * (channels // G)
    weight = conv_weight[0]
    flat_weight = weight
    flipped = jnp.transpose(weight[::-1, ::-1], (0, 1, 3, 2))
    gains = gn_gain[0]
    features = sinusoid(steps, FREQ)
    embedded = jnp.dot(features, emb_weight[0].astype(jnp.float32), precision=lax.Precision.HIGHEST)
    scales = embedded[:, :channels]
    shifts = embedded[:, channels:]
    last = section_count - 1
    carried = images
    kept = None
    for moment in range(section_count):
        inputs = images
        if moment > 0:
            inputs = lax.ppermute(carried, "section", [(moment - 1, moment)])
        if moment == last:
            inputs = (inputs.astype(jnp.float32) + skip.astype(jnp.float32)).astype(jnp.bfloat16)
        output, saved = block_forward(inputs, flat_weight, gains, scales, shifts, cell_count)
        if moment == 0:
            skip = lax.ppermute(output, "section", [(0, last)])
        state = (inputs, saved)
        kept = state if kept is None else keep(section_no == moment, state, kept)
        carried = output
    kept_in, kept_saved = kept
    carried = out_grad
    kept = None
    for moment in range(section_count):
        active = last - moment
        upstream = out_grad
        if moment > 0:
            upstream = lax.ppermute(carried, "section", [(active + 1, active)])
        if active == 0:
            upstream = (upstream.astype(jnp.float32) + skip_grad.astype(jnp.float32)).astype(
                jnp.bfloat16
            )
        d_input, pieces = block_backward(
            upstream, kept_in, kept_saved, flipped, gains, scales, shifts, cell_count
        )
        if moment == 0:
            skip_grad = lax.ppermute(d_input, "section", [(last, 0)])
        state = (upstream, pieces)
        kept = state if kept is None else keep(section_no == active, state, kept)
        carried = d_input
    kept_up, (d_gains, d_scales, d_shifts) = kept
    space_count = lax.axis_size("space")
    space_no = quarter_of(lax.axis_index("space"), space_count)
    patch_rows = 9 * channels // space_count
    flat_patch = patches(kept_saved[2], row_count, col_count).reshape(-1, 9 * channels)
    own_patch = lax.dynamic_slice_in_dim(flat_patch, space_no * patch_rows, patch_rows, axis=1)
    weight_grad = jnp.dot(
        own_patch.T, kept_up.reshape(-1, channels), preferred_element_type=jnp.float32
    )
    emb_rows = FREQ // space_count
    own_features = lax.dynamic_slice_in_dim(features, space_no * emb_rows, emb_rows, axis=1)
    emb_grad = jnp.dot(
        own_features.T,
        jnp.concatenate([d_scales, d_shifts], axis=1),
        precision=lax.Precision.HIGHEST,
    )
    return reduce_grads(weight_grad, d_gains, emb_grad)


def butterfly_scatter(flat, axis):
    count = lax.axis_size(axis)
    index = lax.axis_index(axis)
    step = 1
    while step < count:
        bit = (index // step) % 2
        half = flat.shape[0] // 2
        kept = lax.dynamic_slice_in_dim(flat, bit * half, half, 0)
        sent = lax.dynamic_slice_in_dim(flat, (1 - bit) * half, half, 0)
        flat = kept + lax.ppermute(sent, axis, [(j, j ^ step) for j in range(count)])
        step *= 2
    return flat


def butterfly_sum(flat, axis):
    count = lax.axis_size(axis)
    step = 1
    while step < count:
        flat = flat + lax.ppermute(flat, axis, [(j, j ^ step) for j in range(count)])
        step *= 2
    return flat


def butterfly_gather(flat, axis, steps):
    count = lax.axis_size(axis)
    index = lax.axis_index(axis)
    for step in steps:
        bit = (index // step) % 2
        got = lax.ppermute(flat, axis, [(j, j ^ step) for j in range(count)])
        length = flat.shape[0]
        joined = jnp.zeros((2 * length, *flat.shape[1:]), flat.dtype)
        joined = lax.dynamic_update_slice_in_dim(joined, flat, bit * length, 0)
        flat = lax.dynamic_update_slice_in_dim(joined, got, (1 - bit) * length, 0)
    return flat


def descending(count):
    steps = []
    step = count // 2
    while step >= 1:
        steps.append(step)
        step //= 2
    return steps


def quarter_of(space_no, space_count):
    return (space_no % 2) * (space_count // 2) + space_no // 2


def reduce_grads(weight_grad, gain_grad, emb_grad):
    channels = gain_grad.shape[0]
    parts = [weight_grad, emb_grad.reshape(-1, channels), gain_grad[None]]
    rows = sum(part.shape[0] for part in parts)
    devices = lax.axis_size("dx")
    padded_rows = -(-rows // (8 * devices)) * 8 * devices
    parts.append(jnp.zeros((padded_rows - rows, channels), jnp.float32))
    flat = jnp.concatenate(parts, axis=0)
    flat = butterfly_scatter(flat, "dx")
    flat = butterfly_sum(flat, "dy")
    flat = butterfly_gather(flat.astype(jnp.bfloat16), "dx", descending(lax.axis_size("dx")))
    space_count = lax.axis_size("space")
    flat = butterfly_gather(flat, "space", descending(space_count))
    flat = flat.reshape(space_count, padded_rows, channels).astype(jnp.float32)
    weight_rows = weight_grad.shape[0]
    emb_rows = emb_grad.size // channels
    conv = flat[:, :weight_rows].reshape(1, 3, 3, channels, channels)
    emb = flat[:, weight_rows : weight_rows + emb_rows].reshape(1, emb_grad.shape[0] * space_count, -1)
    gain = flat[0, weight_rows + emb_rows][None]
    return (conv, gain, emb)


def solution(mesh):
    dp_n = mesh.shape["dp"]
    dx_n = 4 if dp_n % 4 == 0 else 1
    mesh = Mesh(
        mesh.devices.reshape(dp_n // dx_n, dx_n, *mesh.devices.shape[1:]),
        ("dy", "dx", "section", "space"),
    )
    data = ("dy", "dx")
    in_specs = (
        P(data, "space", None, None),
        P(data),
        P(data, "space", None, None),
        P("section", None, None, None, None),
        P("section", None),
        P("section", None, None),
    )
    out_specs = (P("section", None, None, None, None), P("section", None), P("section", None, None))
    return jax.shard_map(
        per_device, mesh=mesh, in_specs=in_specs, out_specs=out_specs, check_vma=False
    )
```

```python
import math

import jax
import jax.numpy as jnp
from jax import lax
from jax.sharding import Mesh, PartitionSpec as P

G = 32
FREQ = 256
MICRO = 2


EPS = 1e-05


def from_behind(value, axis, steps):
    count = lax.axis_size(axis)
    initial, last = (max(0, -steps), min(count, count - steps))
    return lax.ppermute(value, axis, [(source, source + steps) for source in range(initial, last)])


def extended(shard, sides, width):
    for axis, dim in sides:
        size, length = (lax.axis_size(axis), shard.shape[dim])
        up = [(i, (i + 1) % size) for i in range(size - 1)]
        down = [(j, i) for i, j in up]
        last = lax.slice_in_dim(shard, length - width, length, axis=dim)
        initial = lax.slice_in_dim(shard, 0, width, axis=dim)
        before = lax.ppermute(last, axis, up)
        after = lax.ppermute(initial, axis, down)
        shard = jnp.concatenate([before, shard, after], axis=dim)
    return shard


def sinusoid(timesteps, feature_n):
    half_n = feature_n // 2
    freqs = jnp.exp(-math.log(10000.0) * jnp.arange(half_n, dtype=jnp.float32) / half_n)
    angles = timesteps.astype(jnp.float32)[:, None] * freqs[None, :]
    return jnp.concatenate([jnp.cos(angles), jnp.sin(angles)], axis=1)


def group_sums(tensor, groups):
    batch_n, height_n, width_n, channels = tensor.shape
    split = tensor.reshape(batch_n, height_n, width_n, groups, channels // groups)
    return (jnp.sum(split, axis=(1, 2, 4)), jnp.sum(split * split, axis=(1, 2, 4)))


def spread(values, channels):
    return jnp.repeat(values, channels // values.shape[1], axis=1)[:, None, None, :]


def normalize(tensor, first_sum, square_sum, gains, scales, shifts, cell_count):
    channels = tensor.shape[3]
    average = first_sum / cell_count
    inverse = lax.rsqrt(square_sum / cell_count - average * average + EPS)
    normed = (tensor - spread(average, channels)) * spread(inverse, channels) * gains
    return normed * (1.0 + scales[:, None, None, :]) + shifts[:, None, None, :]


def patches(padded, height_n, width_n):
    return jnp.concatenate(
        [
            padded[:, vertical : vertical + height_n, lateral : lateral + width_n, :]
            for vertical in range(3)
            for lateral in range(3)
        ],
        axis=3,
    )


def convolve(padded, matrix):
    batch_n, height_p, width_p, channels = padded.shape
    flat = patches(padded, height_p - 2, width_p - 2).reshape(-1, 9 * channels)
    return jnp.dot(flat, matrix, preferred_element_type=jnp.float32).reshape(
        batch_n, height_p - 2, width_p - 2, matrix.shape[1]
    )


def flip_weight(weight):
    channels = weight.shape[2]
    return jnp.transpose(weight[::-1, ::-1], (0, 1, 3, 2)).reshape(9 * channels, channels)


def silu_slope(pre_act):
    sigmoid_v = jax.nn.sigmoid(pre_act)
    return sigmoid_v * (1.0 + pre_act * (1.0 - sigmoid_v))


def pad_columns(tensor):
    return jnp.pad(tensor, ((0, 0), (0, 0), (1, 1), (0, 0)))


def pick(stacked, index):
    return lax.dynamic_index_in_dim(stacked, index, 0, keepdims=False)


def norm_backward(tensor, first_sum, square_sum, gains, scales, shifts, cell_count, d_pre):

    def mapping(tensor_v, first_v, square_v, gains_v, scales_v, shifts_v):
        return normalize(tensor_v, first_v, square_v, gains_v, scales_v, shifts_v, cell_count)

    _, pull_back = jax.vjp(mapping, tensor, first_sum, square_sum, gains, scales, shifts)
    return pull_back(d_pre)


def pad_both(tensor):
    return jnp.pad(tensor, ((0, 0), (1, 1), (1, 1), (0, 0)))


def group_blocks(channels):
    group = jnp.arange(channels) // (channels // G)
    return (group[:, None] == group[None, :]).astype(jnp.float32)


def over_groups(values, blocks):
    return jnp.dot(values, blocks, precision=lax.Precision.HIGHEST)


def normalize_spread(tensor, first_c, square_c, gains, scales, shifts, cell_count):
    average = first_c / cell_count
    inverse = lax.rsqrt(square_c / cell_count - average * average + EPS)
    normed = (tensor - average[:, None, None, :]) * inverse[:, None, None, :] * gains
    return normed * (1.0 + scales[:, None, None, :]) + shifts[:, None, None, :]


def conv_same(tensor, kernel):
    return lax.conv_general_dilated(
        tensor,
        kernel,
        (1, 1),
        ((1, 1), (1, 1)),
        dimension_numbers=("NHWC", "HWIO", "NHWC"),
        preferred_element_type=jnp.float32,
    )


def block_forward(inputs, flat_weight, gains, scales, shifts, cell_count):
    tensor = inputs.astype(jnp.float32)
    blocks = group_blocks(tensor.shape[3])
    first_c = over_groups(jnp.sum(tensor, axis=(1, 2)), blocks)
    square_c = over_groups(jnp.sum(tensor * tensor, axis=(1, 2)), blocks)
    pre_act = normalize_spread(tensor, first_c, square_c, gains, scales, shifts, cell_count)
    activation = jax.nn.silu(pre_act).astype(jnp.bfloat16)
    padded = pad_both(activation)
    output = (tensor + conv_same(activation, flat_weight)).astype(jnp.bfloat16)
    return output, (first_c, square_c, padded, silu_slope(pre_act))


def block_backward(upstream, inputs, saved, flipped, gains, scales, shifts, cell_count):
    first_c, square_c, _, slope = saved
    tensor = inputs.astype(jnp.float32)
    blocks = group_blocks(tensor.shape[3])
    d_act = conv_same(upstream, flipped)
    d_pre = d_act * slope

    def mapping(tensor_v, first_v, square_v, gains_v, scales_v, shifts_v):
        return normalize_spread(tensor_v, first_v, square_v, gains_v, scales_v, shifts_v, cell_count)

    _, pull_back = jax.vjp(mapping, tensor, first_c, square_c, gains, scales, shifts)
    d_tensor, d_first, d_square, d_gains, d_scales, d_shifts = pull_back(d_pre)
    d_first = over_groups(d_first, blocks)[:, None, None, :]
    d_square = over_groups(d_square, blocks)[:, None, None, :]
    d_tensor = d_tensor + d_first + 2.0 * tensor * d_square
    d_input = (upstream.astype(jnp.float32) + d_tensor).astype(jnp.bfloat16)
    return d_input, (d_gains, d_scales, d_shifts)


def keep(flag, new, old):
    return jax.tree.map(lambda a, b: jnp.where(flag, a, b), new, old)


def per_device(images, steps, out_grad, conv_weight, gn_gain, emb_weight):
    section_count = lax.axis_size("section")
    section_no = lax.axis_index("section")
    images = lax.all_gather(images, "space", axis=1, tiled=True)
    out_grad = lax.all_gather(out_grad, "space", axis=1, tiled=True)
    row_count = images.shape[1]
    col_count = images.shape[2]
    channels = images.shape[3]
    cell_count = row_count * col_count * (channels // G)
    weight = conv_weight[0]
    flat_weight = weight
    flipped = jnp.transpose(weight[::-1, ::-1], (0, 1, 3, 2))
    gains = gn_gain[0]
    features = sinusoid(steps, FREQ)
    embedded = jnp.dot(features, emb_weight[0].astype(jnp.float32), precision=lax.Precision.HIGHEST)
    scales = embedded[:, :channels]
    shifts = embedded[:, channels:]
    last = section_count - 1
    carried = images
    kept = None
    for moment in range(section_count):
        inputs = images
        if moment > 0:
            inputs = lax.ppermute(carried, "section", [(moment - 1, moment)])
        if moment == last:
            inputs = (inputs.astype(jnp.float32) + skip.astype(jnp.float32)).astype(jnp.bfloat16)
        output, saved = block_forward(inputs, flat_weight, gains, scales, shifts, cell_count)
        if moment == 0:
            skip = lax.ppermute(output, "section", [(0, last)])
        state = (inputs, saved)
        kept = state if kept is None else keep(section_no == moment, state, kept)
        carried = output
    kept_in, kept_saved = kept
    carried = out_grad
    kept = None
    for moment in range(section_count):
        active = last - moment
        upstream = out_grad
        if moment > 0:
            upstream = lax.ppermute(carried, "section", [(active + 1, active)])
        if active == 0:
            upstream = (upstream.astype(jnp.float32) + skip_grad.astype(jnp.float32)).astype(
                jnp.bfloat16
            )
        d_input, pieces = block_backward(
            upstream, kept_in, kept_saved, flipped, gains, scales, shifts, cell_count
        )
        if moment == 0:
            skip_grad = lax.ppermute(d_input, "section", [(last, 0)])
        state = (upstream, pieces)
        kept = state if kept is None else keep(section_no == active, state, kept)
        carried = d_input
    kept_up, (d_gains, d_scales, d_shifts) = kept
    space_count = lax.axis_size("space")
    space_no = quarter_of(lax.axis_index("space"), space_count)
    patch_rows = 9 * channels // space_count
    flat_patch = patches(kept_saved[2], row_count, col_count).reshape(-1, 9 * channels)
    own_patch = lax.dynamic_slice_in_dim(flat_patch, space_no * patch_rows, patch_rows, axis=1)
    weight_grad = jnp.dot(
        own_patch.T, kept_up.reshape(-1, channels), preferred_element_type=jnp.float32
    )
    emb_rows = FREQ // space_count
    own_features = lax.dynamic_slice_in_dim(features, space_no * emb_rows, emb_rows, axis=1)
    emb_grad = jnp.dot(
        own_features.T,
        jnp.concatenate([d_scales, d_shifts], axis=1),
        precision=lax.Precision.HIGHEST,
    )
    return reduce_grads(weight_grad, d_gains, emb_grad)


def butterfly_scatter(flat, axis):
    count = lax.axis_size(axis)
    index = lax.axis_index(axis)
    step = 1
    while step < count:
        bit = (index // step) % 2
        half = flat.shape[0] // 2
        kept = lax.dynamic_slice_in_dim(flat, bit * half, half, 0)
        sent = lax.dynamic_slice_in_dim(flat, (1 - bit) * half, half, 0)
        flat = kept + lax.ppermute(sent, axis, [(j, j ^ step) for j in range(count)])
        step *= 2
    return flat


def butterfly_sum(flat, axis):
    count = lax.axis_size(axis)
    step = 1
    while step < count:
        flat = flat + lax.ppermute(flat, axis, [(j, j ^ step) for j in range(count)])
        step *= 2
    return flat


def butterfly_gather(flat, axis, steps):
    count = lax.axis_size(axis)
    index = lax.axis_index(axis)
    for step in steps:
        bit = (index // step) % 2
        got = lax.ppermute(flat, axis, [(j, j ^ step) for j in range(count)])
        length = flat.shape[0]
        joined = jnp.zeros((2 * length, *flat.shape[1:]), flat.dtype)
        joined = lax.dynamic_update_slice_in_dim(joined, flat, bit * length, 0)
        flat = lax.dynamic_update_slice_in_dim(joined, got, (1 - bit) * length, 0)
    return flat


def descending(count):
    steps = []
    step = count // 2
    while step >= 1:
        steps.append(step)
        step //= 2
    return steps


def quarter_of(space_no, space_count):
    return (space_no % 2) * (space_count // 2) + space_no // 2


def reduce_grads(weight_grad, gain_grad, emb_grad):
    channels = gain_grad.shape[0]
    parts = [weight_grad, emb_grad.reshape(-1, channels), gain_grad[None]]
    rows = sum(part.shape[0] for part in parts)
    devices = lax.axis_size("dx")
    padded_rows = -(-rows // (8 * devices)) * 8 * devices
    parts.append(jnp.zeros((padded_rows - rows, channels), jnp.float32))
    flat = jnp.concatenate(parts, axis=0)
    flat = butterfly_scatter(flat, "dx")
    flat = butterfly_sum(flat, "dy")
    flat = butterfly_gather(flat.astype(jnp.bfloat16), "dx", descending(lax.axis_size("dx")))
    space_count = lax.axis_size("space")
    flat = butterfly_gather(flat, "space", descending(space_count))
    flat = flat.reshape(space_count, padded_rows, channels).astype(jnp.float32)
    weight_rows = weight_grad.shape[0]
    emb_rows = emb_grad.size // channels
    conv = flat[:, :weight_rows].reshape(1, 3, 3, channels, channels)
    emb = flat[:, weight_rows : weight_rows + emb_rows].reshape(1, emb_grad.shape[0] * space_count, -1)
    gain = flat[0, weight_rows + emb_rows][None]
    return (conv, gain, emb)


def solution(mesh):
    dp_n = mesh.shape["dp"]
    dx_n = 4 if dp_n % 4 == 0 else 1
    mesh = Mesh(
        mesh.devices.reshape(dp_n // dx_n, dx_n, *mesh.devices.shape[1:]),
        ("dy", "dx", "section", "space"),
    )
    data = ("dy", "dx")
    in_specs = (
        P(data, "space", None, None),
        P(data),
        P(data, "space", None, None),
        P("section", None, None, None, None),
        P("section", None),
        P("section", None, None),
    )
    out_specs = (P("section", None, None, None, None), P("section", None), P("section", None, None))
    return jax.shard_map(
        per_device, mesh=mesh, in_specs=in_specs, out_specs=out_specs, check_vma=False
    )
```

```python
import math

import jax
import jax.numpy as jnp
from jax import lax
from jax.sharding import Mesh, PartitionSpec as P

G = 32
FREQ = 256
MICRO = 2


EPS = 1e-05


def from_behind(value, axis, steps):
    count = lax.axis_size(axis)
    initial, last = (max(0, -steps), min(count, count - steps))
    return lax.ppermute(value, axis, [(source, source + steps) for source in range(initial, last)])


def extended(shard, sides, width):
    for axis, dim in sides:
        size, length = (lax.axis_size(axis), shard.shape[dim])
        up = [(i, (i + 1) % size) for i in range(size - 1)]
        down = [(j, i) for i, j in up]
        last = lax.slice_in_dim(shard, length - width, length, axis=dim)
        initial = lax.slice_in_dim(shard, 0, width, axis=dim)
        before = lax.ppermute(last, axis, up)
        after = lax.ppermute(initial, axis, down)
        shard = jnp.concatenate([before, shard, after], axis=dim)
    return shard


def sinusoid(timesteps, feature_n):
    half_n = feature_n // 2
    freqs = jnp.exp(-math.log(10000.0) * jnp.arange(half_n, dtype=jnp.float32) / half_n)
    angles = timesteps.astype(jnp.float32)[:, None] * freqs[None, :]
    return jnp.concatenate([jnp.cos(angles), jnp.sin(angles)], axis=1)


def group_sums(tensor, groups):
    batch_n, height_n, width_n, channels = tensor.shape
    split = tensor.reshape(batch_n, height_n, width_n, groups, channels // groups)
    return (jnp.sum(split, axis=(1, 2, 4)), jnp.sum(split * split, axis=(1, 2, 4)))


def spread(values, channels):
    return jnp.repeat(values, channels // values.shape[1], axis=1)[:, None, None, :]


def normalize(tensor, first_sum, square_sum, gains, scales, shifts, cell_count):
    channels = tensor.shape[3]
    average = first_sum / cell_count
    inverse = lax.rsqrt(square_sum / cell_count - average * average + EPS)
    normed = (tensor - spread(average, channels)) * spread(inverse, channels) * gains
    return normed * (1.0 + scales[:, None, None, :]) + shifts[:, None, None, :]


def patches(padded, height_n, width_n):
    return jnp.concatenate(
        [
            padded[:, vertical : vertical + height_n, lateral : lateral + width_n, :]
            for vertical in range(3)
            for lateral in range(3)
        ],
        axis=3,
    )


def convolve(padded, matrix):
    batch_n, height_p, width_p, channels = padded.shape
    flat = patches(padded, height_p - 2, width_p - 2).reshape(-1, 9 * channels)
    return jnp.dot(flat, matrix, preferred_element_type=jnp.float32).reshape(
        batch_n, height_p - 2, width_p - 2, matrix.shape[1]
    )


def flip_weight(weight):
    channels = weight.shape[2]
    return jnp.transpose(weight[::-1, ::-1], (0, 1, 3, 2)).reshape(9 * channels, channels)


def silu_slope(pre_act):
    sigmoid_v = jax.nn.sigmoid(pre_act)
    return sigmoid_v * (1.0 + pre_act * (1.0 - sigmoid_v))


def pad_columns(tensor):
    return jnp.pad(tensor, ((0, 0), (0, 0), (1, 1), (0, 0)))


def pick(stacked, index):
    return lax.dynamic_index_in_dim(stacked, index, 0, keepdims=False)


def norm_backward(tensor, first_sum, square_sum, gains, scales, shifts, cell_count, d_pre):

    def mapping(tensor_v, first_v, square_v, gains_v, scales_v, shifts_v):
        return normalize(tensor_v, first_v, square_v, gains_v, scales_v, shifts_v, cell_count)

    _, pull_back = jax.vjp(mapping, tensor, first_sum, square_sum, gains, scales, shifts)
    return pull_back(d_pre)


def pad_both(tensor):
    return jnp.pad(tensor, ((0, 0), (1, 1), (1, 1), (0, 0)))


def group_blocks(channels):
    group = jnp.arange(channels) // (channels // G)
    return (group[:, None] == group[None, :]).astype(jnp.float32)


def over_groups(values, blocks):
    return jnp.dot(values, blocks, precision=lax.Precision.HIGHEST)


def normalize_spread(tensor, first_c, square_c, gains, scales, shifts, cell_count):
    average = first_c / cell_count
    inverse = lax.rsqrt(square_c / cell_count - average * average + EPS)
    normed = (tensor - average[:, None, None, :]) * inverse[:, None, None, :] * gains
    return normed * (1.0 + scales[:, None, None, :]) + shifts[:, None, None, :]


def conv_same(tensor, kernel):
    return lax.conv_general_dilated(
        tensor,
        kernel,
        (1, 1),
        ((1, 1), (1, 1)),
        dimension_numbers=("NHWC", "HWIO", "NHWC"),
        preferred_element_type=jnp.float32,
    )


def block_forward(inputs, flat_weight, gains, scales, shifts, cell_count):
    tensor = inputs.astype(jnp.float32)
    blocks = group_blocks(tensor.shape[3])
    first_c = over_groups(jnp.sum(tensor, axis=(1, 2)), blocks)
    square_c = over_groups(jnp.sum(tensor * tensor, axis=(1, 2)), blocks)
    pre_act = normalize_spread(tensor, first_c, square_c, gains, scales, shifts, cell_count)
    activation = jax.nn.silu(pre_act).astype(jnp.bfloat16)
    padded = pad_both(activation)
    output = (tensor + conv_same(activation, flat_weight)).astype(jnp.bfloat16)
    return output, (first_c, square_c, padded)


def block_backward(upstream, inputs, saved, flipped, gains, scales, shifts, cell_count):
    first_c, square_c, _ = saved
    tensor = inputs.astype(jnp.float32)
    blocks = group_blocks(tensor.shape[3])
    pre_act = normalize_spread(tensor, first_c, square_c, gains, scales, shifts, cell_count)
    d_act = conv_same(upstream, flipped)
    d_pre = d_act * silu_slope(pre_act)

    def mapping(tensor_v, first_v, square_v, gains_v, scales_v, shifts_v):
        return normalize_spread(tensor_v, first_v, square_v, gains_v, scales_v, shifts_v, cell_count)

    _, pull_back = jax.vjp(mapping, tensor, first_c, square_c, gains, scales, shifts)
    d_tensor, d_first, d_square, d_gains, d_scales, d_shifts = pull_back(d_pre)
    d_first = over_groups(d_first, blocks)[:, None, None, :]
    d_square = over_groups(d_square, blocks)[:, None, None, :]
    d_tensor = d_tensor + d_first + 2.0 * tensor * d_square
    d_input = (upstream.astype(jnp.float32) + d_tensor).astype(jnp.bfloat16)
    return d_input, (d_gains, d_scales, d_shifts)


def keep(flag, new, old):
    return jax.tree.map(lambda a, b: jnp.where(flag, a, b), new, old)


def per_device(images, steps, out_grad, conv_weight, gn_gain, emb_weight):
    section_count = lax.axis_size("section")
    section_no = lax.axis_index("section")
    images = lax.all_gather(images, "space", axis=1, tiled=True)
    out_grad = lax.all_gather(out_grad, "space", axis=1, tiled=True)
    row_count = images.shape[1]
    col_count = images.shape[2]
    channels = images.shape[3]
    cell_count = row_count * col_count * (channels // G)
    weight = conv_weight[0]
    flat_weight = weight
    flipped = jnp.transpose(weight[::-1, ::-1], (0, 1, 3, 2))
    gains = gn_gain[0]
    features = sinusoid(steps, FREQ)
    embedded = jnp.dot(features, emb_weight[0].astype(jnp.float32), precision=lax.Precision.HIGHEST)
    scales = embedded[:, :channels]
    shifts = embedded[:, channels:]
    last = section_count - 1
    carried = images
    kept = None
    for moment in range(section_count):
        inputs = images
        if moment > 0:
            inputs = lax.ppermute(carried, "section", [(moment - 1, moment)])
        if moment == last:
            inputs = (inputs.astype(jnp.float32) + skip.astype(jnp.float32)).astype(jnp.bfloat16)
        output, saved = block_forward(inputs, flat_weight, gains, scales, shifts, cell_count)
        if moment == 0:
            skip = lax.ppermute(output, "section", [(0, last)])
        state = (inputs, saved)
        kept = state if kept is None else keep(section_no == moment, state, kept)
        carried = output
    kept_in, kept_saved = kept
    carried = out_grad
    kept = None
    for moment in range(section_count):
        active = last - moment
        upstream = out_grad
        if moment > 0:
            upstream = lax.ppermute(carried, "section", [(active + 1, active)])
        if active == 0:
            upstream = (upstream.astype(jnp.float32) + skip_grad.astype(jnp.float32)).astype(
                jnp.bfloat16
            )
        d_input, pieces = block_backward(
            upstream, kept_in, kept_saved, flipped, gains, scales, shifts, cell_count
        )
        if moment == 0:
            skip_grad = lax.ppermute(d_input, "section", [(last, 0)])
        state = (upstream, pieces)
        kept = state if kept is None else keep(section_no == active, state, kept)
        carried = d_input
    kept_up, (d_gains, d_scales, d_shifts) = kept
    space_count = lax.axis_size("space")
    space_no = quarter_of(lax.axis_index("space"), space_count)
    patch_rows = 9 * channels // space_count
    flat_patch = patches(kept_saved[2], row_count, col_count).reshape(-1, 9 * channels)
    own_patch = lax.dynamic_slice_in_dim(flat_patch, space_no * patch_rows, patch_rows, axis=1)
    weight_grad = jnp.dot(
        own_patch.T, kept_up.reshape(-1, channels), preferred_element_type=jnp.float32
    )
    emb_rows = FREQ // space_count
    own_features = lax.dynamic_slice_in_dim(features, space_no * emb_rows, emb_rows, axis=1)
    emb_grad = jnp.dot(
        own_features.T,
        jnp.concatenate([d_scales, d_shifts], axis=1),
        precision=lax.Precision.HIGHEST,
    )
    return reduce_grads(weight_grad, d_gains, emb_grad)


def butterfly_scatter(flat, axis):
    count = lax.axis_size(axis)
    index = lax.axis_index(axis)
    step = 1
    while step < count:
        bit = (index // step) % 2
        half = flat.shape[0] // 2
        kept = lax.dynamic_slice_in_dim(flat, bit * half, half, 0)
        sent = lax.dynamic_slice_in_dim(flat, (1 - bit) * half, half, 0)
        flat = kept + lax.ppermute(sent, axis, [(j, j ^ step) for j in range(count)])
        step *= 2
    return flat


def butterfly_sum(flat, axis):
    count = lax.axis_size(axis)
    step = 1
    while step < count:
        flat = flat + lax.ppermute(flat, axis, [(j, j ^ step) for j in range(count)])
        step *= 2
    return flat


def butterfly_gather(flat, axis, steps):
    count = lax.axis_size(axis)
    index = lax.axis_index(axis)
    for step in steps:
        bit = (index // step) % 2
        got = lax.ppermute(flat, axis, [(j, j ^ step) for j in range(count)])
        length = flat.shape[0]
        joined = jnp.concatenate([flat, flat])
        flat = lax.dynamic_update_slice_in_dim(joined, got, (1 - bit) * length, 0)
    return flat


def descending(count):
    steps = []
    step = count // 2
    while step >= 1:
        steps.append(step)
        step //= 2
    return steps


def quarter_of(space_no, space_count):
    return (space_no % 2) * (space_count // 2) + space_no // 2


def reduce_grads(weight_grad, gain_grad, emb_grad):
    channels = gain_grad.shape[0]
    parts = [weight_grad, emb_grad.reshape(-1, channels), gain_grad[None]]
    rows = sum(part.shape[0] for part in parts)
    devices = lax.axis_size("dx")
    padded_rows = -(-rows // (8 * devices)) * 8 * devices
    parts.append(jnp.zeros((padded_rows - rows, channels), jnp.float32))
    flat = jnp.concatenate(parts, axis=0)
    flat = butterfly_scatter(flat, "dx")
    flat = butterfly_sum(flat, "dy")
    flat = butterfly_gather(flat.astype(jnp.bfloat16), "dx", descending(lax.axis_size("dx")))
    space_count = lax.axis_size("space")
    flat = butterfly_gather(flat, "space", descending(space_count))
    flat = flat.reshape(space_count, padded_rows, channels).astype(jnp.float32)
    weight_rows = weight_grad.shape[0]
    emb_rows = emb_grad.size // channels
    conv = flat[:, :weight_rows].reshape(1, 3, 3, channels, channels)
    emb = flat[:, weight_rows : weight_rows + emb_rows].reshape(1, emb_grad.shape[0] * space_count, -1)
    gain = flat[0, weight_rows + emb_rows][None]
    return (conv, gain, emb)


def solution(mesh):
    dp_n = mesh.shape["dp"]
    dx_n = 4 if dp_n % 4 == 0 else 1
    mesh = Mesh(
        mesh.devices.reshape(dp_n // dx_n, dx_n, *mesh.devices.shape[1:]),
        ("dy", "dx", "section", "space"),
    )
    data = ("dy", "dx")
    in_specs = (
        P(data, "space", None, None),
        P(data),
        P(data, "space", None, None),
        P("section", None, None, None, None),
        P("section", None),
        P("section", None, None),
    )
    out_specs = (P("section", None, None, None, None), P("section", None), P("section", None, None))
    return jax.shard_map(
        per_device, mesh=mesh, in_specs=in_specs, out_specs=out_specs, check_vma=False
    )
```
